128 devices in a mesh: gx: 16 (over y_hi, z, core), gy: 8 (over x, y_lo).
Axes of the slice: x: 4, y: 4 (y_hi: 2, y_lo: 2; y = y_hi * 2 + y_lo), z: 4, core: 2. Of those that a mesh axis runs over, the one named last changes fastest.
Arguments:
- payload: float32 [4, 2097152], P(None, ('gx', 'gy'))
- cells: int32 [3, 2097152], P(None, ('gx', 'gy')), may hold values from 0 to 127, as said below
- counts: int32 [128, 9], P(('gx', 'gy')), may hold values from 128 to 12596, as said below
Outputs:
- scalar_field: float32 [8, 256, 1024], P(None, 'gx', 'gy')
- momentum: float32 [3, 8, 256, 1024], P(None, None, 'gx', 'gy')
The draws below stay inside these ranges and needn't reach their ends.
Inputs may be any that keep to these rules, and one draw needn't show every extreme that they name: Rows of a tile are grouped by direction in the order of counts' columns. A face direction holds at most 2048 rows of a tile and a corner direction at most 512; each of these bounds is reached in some tile. A row of counts sums to 16384. cells[0] is below 8, cells[1] below 16, cells[2] below 128. A particle moving +x lands in x layers 0 to 1 of its destination tile, one moving -x in layers 14 to 15; likewise +y in y layers 0 to 15 and -y in 112 to 127; corner directions are bound in both; otherwise any cell.
All inputs are finite; a program needn't handle non-finite values.
Results may differ from the reference program's by a relative error of at most 0.000054.
Values sent between devices are 32-bit elements; how exact they have to be, the bound alone decides.
No kernel may reach another device: no remote copies, remote signals or barrier semaphores. Data moves between devices by JAX's collectives and lax.ppermute only.
A program may use at most 64 MiB of HBM per device.

```python
import jax
import jax.numpy as jnp

CX = 16
CY = 128
NZ = 8
SWEEPS = 4
PART = 16384
CAP_F = 2048
CAP_D = 512
MX = 2
MY = 16
TILES = 128
PARTS_ALL = 2097152
NX = 256
NY = 1024
N_GX = 16
N_GY = 8


def tile_counts(key):
    base = jax.random.fold_in(key, 7)
    key_face, key_corner, key_topf, key_topc, key_low = jax.random.split(base, 5)
    low_face = 2 * CAP_F // 5
    low_corner = CAP_D // 4
    face_counts = jax.random.randint(key_face, (TILES, 4), low_face, CAP_F + 1)
    corner_counts = jax.random.randint(key_corner, (TILES, 4), low_corner, CAP_D + 1)
    low_tile = jax.random.randint(key_low, (), 0, TILES)
    top_face = (low_tile + 1 + jax.random.randint(key_topf, (4,), 0, TILES - 1)) % TILES
    top_corner = (low_tile + 1 + jax.random.randint(key_topc, (4,), 0, TILES - 1)) % TILES
    tile_rows = jnp.arange(TILES)[:, None]
    face_counts = jnp.where(tile_rows == low_tile, low_face, face_counts)
    corner_counts = jnp.where(tile_rows == low_tile, low_corner, corner_counts)
    face_counts = jnp.where(tile_rows == top_face[None, :], CAP_F, face_counts)
    corner_counts = jnp.where(tile_rows == top_corner[None, :], CAP_D, corner_counts)
    staying = PART - jnp.sum(face_counts, axis=1) - jnp.sum(corner_counts, axis=1)
    return jnp.concatenate([face_counts, corner_counts, staying[:, None]], axis=1).astype(jnp.int32)


def draw_counts(key, part):
    return tile_counts(key)


def draw_cells(key, part):
    counts = tile_counts(key)
    limits = jnp.cumsum(counts, axis=1)
    position = jnp.arange(PART, dtype=jnp.int32)
    direction = jnp.zeros((TILES, PART), jnp.int32)
    for edge in range(8):
        direction = direction + (position[None, :] >= limits[:, edge:edge + 1]).astype(jnp.int32)
    step_x = ((direction == 0) | (direction == 4) | (direction == 5)).astype(jnp.int32) - ((direction == 1) | (direction == 6) | (direction == 7)).astype(jnp.int32)
    step_y = ((direction == 2) | (direction == 4) | (direction == 6)).astype(jnp.int32) - ((direction == 3) | (direction == 5) | (direction == 7)).astype(jnp.int32)
    base = jax.random.fold_in(key, 13)
    key_i, key_j, key_k = jax.random.split(base, 3)
    raw_i = jax.random.randint(key_i, (TILES, PART), 0, 2 ** 20)
    raw_j = jax.random.randint(key_j, (TILES, PART), 0, 2 ** 20)
    depth_k = jax.random.randint(key_k, (TILES, PART), 0, NZ)
    start_i = jnp.where(step_x == -1, CX - MX, 0)
    span_i = jnp.where(step_x == 0, CX, MX)
    start_j = jnp.where(step_y == -1, CY - MY, 0)
    span_j = jnp.where(step_y == 0, CY, MY)
    place_i = start_i + raw_i % span_i
    place_j = start_j + raw_j % span_j
    return jnp.stack([depth_k.reshape(-1), place_i.reshape(-1), place_j.reshape(-1)], axis=0).astype(jnp.int32)


def draw_payload(key, part):
    key_mass, key_speed = jax.random.split(jax.random.fold_in(key, 29))
    masses = jnp.exp(jax.random.uniform(key_mass, (1, PARTS_ALL), jnp.float32, jnp.log(0.3), jnp.log(3.0)))
    speeds = jnp.clip(jax.random.normal(key_speed, (3, PARTS_ALL), jnp.float32), -4.0, 4.0)
    return jnp.concatenate([masses, speeds], axis=0).astype(jnp.float32)


def setup_inputs(seed: int = 0) -> dict:
    streams_of = jax.random.split(jax.random.key(seed), 4)
    payload = draw_payload(jax.random.fold_in(streams_of[3], 71), 0)
    cells = draw_cells(jax.random.fold_in(streams_of[3], 71), 0)
    counts = draw_counts(jax.random.fold_in(streams_of[3], 71), 0)
    return dict(payload=payload, cells=cells, counts=counts)


SCREENING = 0.5
CUBIC_TERM = 0.3
COUPLING = 1.5
SMOOTHING = 0.1
BACKGROUND = 1.0


def row_directions(counts):
    limits = jnp.cumsum(counts, axis=1)
    position = jnp.arange(PART, dtype=jnp.int32)
    direction = jnp.zeros((TILES, PART), jnp.int32)
    for edge in range(8):
        direction = direction + (position[None, :] >= limits[:, edge:edge + 1]).astype(jnp.int32)
    return direction.reshape(-1)


def direction_steps(direction):
    step_x = ((direction == 0) | (direction == 4) | (direction == 5)).astype(jnp.int32) - ((direction == 1) | (direction == 6) | (direction == 7)).astype(jnp.int32)
    step_y = ((direction == 2) | (direction == 4) | (direction == 6)).astype(jnp.int32) - ((direction == 3) | (direction == 5) | (direction == 7)).astype(jnp.int32)
    return step_x, step_y


def neighbours(field):
    stacked = jnp.pad(field, ((1, 1), (0, 0), (0, 0)))
    return stacked[2:] + stacked[:-2] + jnp.roll(field, -1, 1) + jnp.roll(field, 1, 1) + jnp.roll(field, -1, 2) + jnp.roll(field, 1, 2)


def reference(payload, cells, counts):
    direction = row_directions(counts)
    step_x, step_y = direction_steps(direction)
    tile_index = jnp.arange(PARTS_ALL, dtype=jnp.int32) // PART
    tile_x = tile_index // N_GY
    tile_y = tile_index % N_GY
    depth_k = cells[0]
    place_i = cells[1]
    place_j = cells[2]
    global_x = ((tile_x + step_x) % N_GX) * CX + place_i
    global_y = ((tile_y + step_y) % N_GY) * CY + place_j
    flat_index = (depth_k * NX + global_x) * NY + global_y
    masses = payload[0]
    density = jnp.zeros((NZ * NX * NY,), jnp.float32).at[flat_index].add(masses).reshape(NZ, NX, NY)
    moments = []
    for component in range(3):
        moments.append(jnp.zeros((NZ * NX * NY,), jnp.float32).at[flat_index].add(masses * payload[component + 1]).reshape(NZ, NX, NY))
    momentum = jnp.stack(moments, axis=0)
    smoothed = density + SMOOTHING * (neighbours(density) - 6.0 * density)
    source = COUPLING * (smoothed - BACKGROUND)
    parity = (jnp.arange(NZ, dtype=jnp.int32)[:, None, None] + jnp.arange(NX, dtype=jnp.int32)[None, :, None] + jnp.arange(NY, dtype=jnp.int32)[None, None, :]) % 2
    scalar_field = jnp.zeros((NZ, NX, NY), jnp.float32)
    for sweep_no in range(SWEEPS):
        for colour in (0, 1):
            middle = scalar_field
            residual = neighbours(middle) - 6.0 * middle - SCREENING * middle - CUBIC_TERM * middle * middle * middle - source
            slope = -6.0 - SCREENING - 3.0 * CUBIC_TERM * middle * middle
            scalar_field = jnp.where(parity == colour, middle - residual / slope, middle)
    return scalar_field, momentum
```

```python
import jax
import jax.numpy as jnp
from jax import lax
from jax.experimental import pallas as pl
from jax.experimental.pallas import tpu as pltpu
from jax.sharding import PartitionSpec as P

CX = 16
CY = 128
NZ = 8
SWEEPS = 4
PART = 16384
CAP_F = 2048
CAP_D = 512


SCREENING = 0.5
CUBIC_TERM = 0.3
COUPLING = 1.5
SMOOTHING = 0.1
BACKGROUND = 1.0

HALO = 2 * SWEEPS
ROWS = 64
COLS = 256
SPLITS = 3
BLOCK = 1024

STEPS = ((1, 0), (-1, 0), (0, 1), (0, -1), (1, 1), (1, -1), (-1, 1), (-1, -1))


def deposit_kernel(first_ref, x_ref, o_ref):
    step = pl.program_id(0)

    @pl.when(step == 0)
    def _():
        o_ref[...] = jnp.zeros(o_ref.shape, o_ref.dtype)

    @pl.when(step >= first_ref[0])
    def _():
        x = x_ref[...]
        vals = x[0:4]
        cell = x[4:5].astype(jnp.int32)
        row = lax.shift_right_arithmetic(cell, 8)
        col = lax.bitwise_and(cell, COLS - 1)
        hi = vals.astype(jnp.bfloat16)
        rest = vals - hi.astype(jnp.float32)
        mid = rest.astype(jnp.bfloat16)
        lo = (rest - mid.astype(jnp.float32)).astype(jnp.bfloat16)
        parts = [p.astype(jnp.float32)[c : c + 1] for p in (hi, mid, lo) for c in range(4)]
        width = x.shape[1]
        row_hot = (lax.broadcasted_iota(jnp.int32, (ROWS, width), 0) == row).astype(jnp.float32)
        left = jnp.concatenate(
            [(row_hot * part).astype(jnp.bfloat16) for part in parts], axis=0
        )
        right = (lax.broadcasted_iota(jnp.int32, (COLS, width), 0) == col).astype(jnp.bfloat16)
        o_ref[...] += lax.dot_general(
            left, right, (((1,), (1,)), ((), ())), preferred_element_type=jnp.float32
        )


def deposit(packed, first_block):
    count = packed.shape[1] // BLOCK
    out = pl.pallas_call(
        deposit_kernel,
        grid_spec=pltpu.PrefetchScalarGridSpec(
            num_scalar_prefetch=1,
            grid=(count,),
            in_specs=[pl.BlockSpec((5, BLOCK), lambda b, first: (0, jnp.maximum(b, first[0])))],
            out_specs=pl.BlockSpec((4 * SPLITS * ROWS, COLS), lambda b, first: (0, 0)),
        ),
        out_shape=jax.ShapeDtypeStruct((4 * SPLITS * ROWS, COLS), jnp.float32),
        compiler_params=pltpu.CompilerParams(dimension_semantics=("arbitrary",)),
    )(first_block, packed)
    return out.reshape(SPLITS, 4, ROWS * COLS)


def combine(total):
    summed = (total[0] + total[1]) + total[2]
    return summed.reshape(4, NZ, CX, CY)


def extended(cells, sides, width):
    for axis, dim in sides:
        count = lax.axis_size(axis)
        head = lax.slice_in_dim(cells, 0, width, axis=dim)
        tail = lax.slice_in_dim(cells, cells.shape[dim] - width, cells.shape[dim], axis=dim)
        cells = jnp.concatenate(
            [
                lax.ppermute(tail, axis, [(i, (i + 1) % count) for i in range(count)]),
                cells,
                lax.ppermute(head, axis, [((i + 1) % count, i) for i in range(count)]),
            ],
            axis=dim,
        )
    return cells


def neighbours(bordered):
    middle = bordered[:, 1:-1, 1:-1]
    stacked = jnp.pad(middle, ((1, 1), (0, 0), (0, 0)))
    return (
        stacked[2:]
        + stacked[:-2]
        + bordered[:, 2:, 1:-1]
        + bordered[:, :-2, 1:-1]
        + bordered[:, 1:-1, 2:]
        + bordered[:, 1:-1, :-2]
    )


def smooth_source(bordered):
    middle = bordered[:, 1:-1, 1:-1]
    smoothed = middle + SMOOTHING * (neighbours(bordered) - 6.0 * middle)
    return COUPLING * (smoothed - BACKGROUND)


def relax_cells(bordered, source, colour):
    middle = bordered[:, 1:-1, 1:-1]
    residual = (
        neighbours(bordered)
        - 6.0 * middle
        - SCREENING * middle
        - CUBIC_TERM * middle * middle * middle
        - source
    )
    slope = -6.0 - SCREENING - 3.0 * CUBIC_TERM * middle * middle
    shape = middle.shape
    parity = (
        lax.broadcasted_iota(jnp.int32, shape, 0)
        + lax.broadcasted_iota(jnp.int32, shape, 1)
        + lax.broadcasted_iota(jnp.int32, shape, 2)
    ) % 2
    return jnp.where(parity == colour, middle - residual / slope, middle)


def crop(field, width):
    return field[:, width:-width, width:-width] if width else field


def shards(payload, cells, counts):
    tallies = counts[0]
    limits = jnp.cumsum(tallies)
    starts = limits - tallies
    masses = payload[0]
    values = jnp.concatenate([masses[None, :], masses[None, :] * payload[1:]], axis=0)
    flat = (cells[0] * CX + cells[1]) * CY + cells[2]
    position = jnp.arange(PART, dtype=jnp.int32)

    gx = lax.axis_size("gx")
    gy = lax.axis_size("gy")
    sends = []
    for which, (sx, sy) in enumerate(STEPS):
        capacity = CAP_F if which < 4 else CAP_D
        block = lax.dynamic_slice_in_dim(values, starts[which], capacity, 1)
        target = lax.dynamic_slice_in_dim(flat, starts[which], capacity, 0)
        living = jnp.arange(capacity, dtype=jnp.int32) < tallies[which]
        target = jnp.where(living, target, -1).astype(jnp.float32)
        packed = jnp.concatenate([block, target[None, :]], axis=0)
        route = []
        for ix in range(gx):
            for iy in range(gy):
                route.append((ix * gy + iy, ((ix + sx) % gx) * gy + (iy + sy) % gy))
        sends.append(lax.ppermute(packed, ("gx", "gy"), route))

    staying = jnp.where(position >= starts[8], flat, -1).astype(jnp.float32)
    local = jnp.concatenate([values, staying[None, :]], axis=0)
    first_local = (starts[8] // BLOCK).astype(jnp.int32).reshape(1)
    total = deposit(local, first_local)
    arrived = jnp.concatenate(sends, axis=1)
    total = total + deposit(arrived, jnp.zeros((1,), jnp.int32))
    interior = combine(total)
    density = interior[0]
    momentum = interior[1:]

    padded = extended(density, (("gx", 1), ("gy", 2)), HALO)
    source = smooth_source(padded)
    field = jnp.zeros(source.shape, jnp.float32)
    bordered = jnp.pad(field, ((0, 0), (1, 1), (1, 1)))
    step = 0
    for sweep_no in range(SWEEPS):
        for colour in (0, 1):
            field = relax_cells(bordered, crop(source, step), colour)
            step += 1
            bordered = field
    scalar_field = field
    return (scalar_field, momentum)


def solution(mesh):
    placed = (P(None, ("gx", "gy")), P(None, ("gx", "gy")), P(("gx", "gy"), None))
    return jax.shard_map(
        shards,
        mesh=mesh,
        in_specs=placed,
        out_specs=(P(None, "gx", "gy"), P(None, None, "gx", "gy")),
        check_vma=False,
    )
```

```python
import jax
import jax.numpy as jnp
from jax import lax
from jax.experimental import pallas as pl
from jax.experimental.pallas import tpu as pltpu
from jax.sharding import PartitionSpec as P

CX = 16
CY = 128
NZ = 8
SWEEPS = 4
PART = 16384
CAP_F = 2048
CAP_D = 512


SCREENING = 0.5
CUBIC_TERM = 0.3
COUPLING = 1.5
SMOOTHING = 0.1
BACKGROUND = 1.0

HALO = 2 * SWEEPS
ROWS = 64
COLS = 256
SPLITS = 3
LOCAL_BLOCK = 1024
ARRIVED_BLOCK = 512
WIDE_X = 2 * CX
WIDE_Y = 2 * CY

STEPS = ((1, 0), (-1, 0), (0, 1), (0, -1), (1, 1), (1, -1), (-1, 1), (-1, -1))


def local_direction(step):
    return 8


def arrived_direction(step):
    face_blocks = CAP_F // ARRIVED_BLOCK
    return jnp.where(step < 4 * face_blocks, step // face_blocks, step - 4 * face_blocks + 4)


def deposit_body(direction_of, first_ref, x_ref, acc_ref, o_ref):
    step = pl.program_id(0)

    @pl.when(step == 0)
    def _():
        if acc_ref is None:
            o_ref[...] = jnp.zeros(o_ref.shape, o_ref.dtype)
        else:
            o_ref[...] = acc_ref[...]

    @pl.when(step >= first_ref[0])
    def _():
        x = x_ref[...]
        vals = x[0:4]
        cell = x[4:5].astype(jnp.int32) - direction_of(step) * PART
        cell = jnp.where((cell >= 0) & (cell < PART), cell, -1)
        row = lax.shift_right_arithmetic(cell, 8)
        col = lax.bitwise_and(cell, COLS - 1)
        hi = vals.astype(jnp.bfloat16)
        rest = vals - hi.astype(jnp.float32)
        mid = rest.astype(jnp.bfloat16)
        lo = (rest - mid.astype(jnp.float32)).astype(jnp.bfloat16)
        parts = [p.astype(jnp.float32)[c : c + 1] for p in (hi, mid, lo) for c in range(4)]
        width = x.shape[1]
        row_hot = (lax.broadcasted_iota(jnp.int32, (ROWS, width), 0) == row).astype(jnp.float32)
        left = jnp.concatenate([(row_hot * part).astype(jnp.bfloat16) for part in parts], axis=0)
        right = (lax.broadcasted_iota(jnp.int32, (COLS, width), 0) == col).astype(jnp.bfloat16)
        o_ref[...] += lax.dot_general(
            left, right, (((1,), (1,)), ((), ())), preferred_element_type=jnp.float32
        )


def deposit(packed, first_block, block, direction_of, acc=None):
    count = packed.shape[1] // block
    shape = (4 * SPLITS * ROWS, COLS)
    in_specs = [pl.BlockSpec((5, block), lambda b, first: (0, jnp.maximum(b, first[0])))]
    operands = [first_block, packed]
    aliases = {}
    if acc is None:
        kernel = lambda f, x, o: deposit_body(direction_of, f, x, None, o)
    else:
        kernel = lambda f, x, a, o: deposit_body(direction_of, f, x, a, o)
        in_specs.append(pl.BlockSpec(shape, lambda b, first: (0, 0)))
        operands.append(acc)
        aliases = {2: 0}
    return pl.pallas_call(
        kernel,
        grid_spec=pltpu.PrefetchScalarGridSpec(
            num_scalar_prefetch=1,
            grid=(count,),
            in_specs=in_specs,
            out_specs=pl.BlockSpec(shape, lambda b, first: (0, 0)),
        ),
        out_shape=jax.ShapeDtypeStruct(shape, jnp.float32),
        input_output_aliases=aliases,
        compiler_params=pltpu.CompilerParams(dimension_semantics=("arbitrary",)),
    )(*operands)


def combine(total):
    total = total.reshape(SPLITS, 4, ROWS * COLS)
    summed = (total[0] + total[1]) + total[2]
    return summed.reshape(4, NZ, CX, CY)


def shifted(block, axis, route_to):
    count = lax.axis_size(axis)
    return lax.ppermute(block, axis, [(i, (i + route_to) % count) for i in range(count)])


def bordered_density(density):
    head = density[:, :HALO, :]
    tail = density[:, CX - HALO :, :]
    wide = jnp.concatenate([density, shifted(head, "gx", -1), shifted(tail, "gx", 1)], axis=1)
    head = wide[:, :, :HALO]
    tail = wide[:, :, CY - HALO :]
    gap = jnp.zeros((NZ, WIDE_X, WIDE_Y - CY - 2 * HALO), jnp.float32)
    return jnp.concatenate([wide, shifted(head, "gy", -1), gap, shifted(tail, "gy", 1)], axis=2)


def near(v):
    flat = jnp.zeros((1,) + v.shape[1:], v.dtype)
    up = jnp.concatenate([v[1:], flat], axis=0)
    down = jnp.concatenate([flat, v[:-1]], axis=0)
    return (
        up
        + down
        + pltpu.roll(v, WIDE_X - 1, 1)
        + pltpu.roll(v, 1, 1)
        + pltpu.roll(v, WIDE_Y - 1, 2)
        + pltpu.roll(v, 1, 2)
    )


def relax_kernel(d_ref, o_ref):
    density = d_ref[...]
    source = COUPLING * ((density + SMOOTHING * (near(density) - 6.0 * density)) - BACKGROUND)
    shape = density.shape
    parity = (
        lax.broadcasted_iota(jnp.int32, shape, 0)
        + lax.broadcasted_iota(jnp.int32, shape, 1)
        + lax.broadcasted_iota(jnp.int32, shape, 2)
    ) % 2
    field = jnp.zeros(shape, jnp.float32)
    for sweep_no in range(SWEEPS):
        for colour in (0, 1):
            middle = field
            residual = (
                near(middle)
                - 6.0 * middle
                - SCREENING * middle
                - CUBIC_TERM * middle * middle * middle
                - source
            )
            slope = -6.0 - SCREENING - 3.0 * CUBIC_TERM * middle * middle
            field = jnp.where(parity == colour, middle - residual / slope, middle)
    o_ref[...] = field[:, :CX, :CY]


def relax(bordered):
    return pl.pallas_call(
        relax_kernel,
        out_shape=jax.ShapeDtypeStruct((NZ, CX, CY), jnp.float32),
    )(bordered)


def shards(payload, cells, counts):
    tallies = counts[0]
    limits = jnp.cumsum(tallies)
    starts = limits - tallies
    masses = payload[0]
    position = jnp.arange(PART, dtype=jnp.int32)
    direction = jnp.zeros((PART,), jnp.int32)
    for edge in range(8):
        direction = direction + (position >= limits[edge]).astype(jnp.int32)
    flat = (cells[0] * CX + cells[1]) * CY + cells[2]
    tag = (direction * PART + flat).astype(jnp.float32)
    packed = jnp.concatenate([masses[None, :], masses[None, :] * payload[1:], tag[None, :]], axis=0)

    gx = lax.axis_size("gx")
    gy = lax.axis_size("gy")
    sends = []
    for which, (sx, sy) in enumerate(STEPS):
        capacity = CAP_F if which < 4 else CAP_D
        block = lax.dynamic_slice_in_dim(packed, starts[which], capacity, 1)
        route = []
        for ix in range(gx):
            for iy in range(gy):
                route.append((ix * gy + iy, ((ix + sx) % gx) * gy + (iy + sy) % gy))
        sends.append(lax.ppermute(block, ("gx", "gy"), route))

    first_local = (starts[8] // LOCAL_BLOCK).astype(jnp.int32).reshape(1)
    total = deposit(packed, first_local, LOCAL_BLOCK, local_direction)
    arrived = jnp.concatenate(sends, axis=1)
    total = deposit(arrived, jnp.zeros((1,), jnp.int32), ARRIVED_BLOCK, arrived_direction, total)
    interior = combine(total)
    density = interior[0]
    momentum = interior[1:]
    scalar_field = relax(bordered_density(density))
    return (scalar_field, momentum)


def solution(mesh):
    placed = (P(None, ("gx", "gy")), P(None, ("gx", "gy")), P(("gx", "gy"), None))
    return jax.shard_map(
        shards,
        mesh=mesh,
        in_specs=placed,
        out_specs=(P(None, "gx", "gy"), P(None, None, "gx", "gy")),
        check_vma=False,
    )
```

```python
import jax
import jax.numpy as jnp
from jax import lax
from jax.experimental import pallas as pl
from jax.experimental.pallas import tpu as pltpu
from jax.sharding import PartitionSpec as P

CX = 16
CY = 128
NZ = 8
SWEEPS = 4
PART = 16384
CAP_F = 2048
CAP_D = 512


SCREENING = 0.5
CUBIC_TERM = 0.3
COUPLING = 1.5
SMOOTHING = 0.1
BACKGROUND = 1.0

HALO = 2 * SWEEPS
ROWS = 64
COLS = 256
SPLITS = 3
BLOCK = 2048
WIDE_X = 2 * CX
WIDE_Y = 2 * CY

STEPS = ((1, 0), (-1, 0), (0, 1), (0, -1), (1, 1), (1, -1), (-1, 1), (-1, -1))


def deposit_body(first_ref, p_ref, c_ref, acc_ref, o_ref):
    step = pl.program_id(0)

    @pl.when(step == 0)
    def _():
        if acc_ref is None:
            o_ref[...] = jnp.zeros(o_ref.shape, o_ref.dtype)
        else:
            o_ref[...] = acc_ref[...]

    @pl.when(step * BLOCK + BLOCK > first_ref[0])
    def _():
        p = p_ref[...].astype(jnp.float32)
        c = c_ref[...].astype(jnp.int32)
        width = p.shape[1]
        masses = p[0:1]
        vals = jnp.concatenate([masses, masses * p[1:4]], axis=0)
        cell = (c[0:1] * CX + c[1:2]) * CY + c[2:3]
        position = step * BLOCK + lax.broadcasted_iota(jnp.int32, (1, width), 1)
        cell = jnp.where(position >= first_ref[0], cell, -1)
        row = lax.shift_right_arithmetic(cell, 8)
        col = lax.bitwise_and(cell, COLS - 1)
        hi = vals.astype(jnp.bfloat16)
        rest = vals - hi.astype(jnp.float32)
        mid = rest.astype(jnp.bfloat16)
        lo = (rest - mid.astype(jnp.float32)).astype(jnp.bfloat16)
        parts = [q.astype(jnp.float32)[e : e + 1] for q in (hi, mid, lo) for e in range(4)]
        row_hot = (lax.broadcasted_iota(jnp.int32, (ROWS, width), 0) == row).astype(jnp.float32)
        left = jnp.concatenate([(row_hot * part).astype(jnp.bfloat16) for part in parts], axis=0)
        right = (lax.broadcasted_iota(jnp.int32, (COLS, width), 0) == col).astype(jnp.bfloat16)
        o_ref[...] += lax.dot_general(
            left, right, (((1,), (1,)), ((), ())), preferred_element_type=jnp.float32
        )


def deposit(values, targets, first, acc=None):
    count = values.shape[1] // BLOCK
    shape = (4 * SPLITS * ROWS, COLS)
    pick = lambda b, f: (0, jnp.maximum(b, f[0] // BLOCK))
    in_specs = [pl.BlockSpec((4, BLOCK), pick), pl.BlockSpec((3, BLOCK), pick)]
    operands = [first, values, targets]
    aliases = {}
    if acc is None:
        kernel = lambda f, p, c, o: deposit_body(f, p, c, None, o)
    else:
        kernel = deposit_body
        in_specs.append(pl.BlockSpec(shape, lambda b, f: (0, 0)))
        operands.append(acc)
        aliases = {3: 0}
    return pl.pallas_call(
        kernel,
        grid_spec=pltpu.PrefetchScalarGridSpec(
            num_scalar_prefetch=1,
            grid=(count,),
            in_specs=in_specs,
            out_specs=pl.BlockSpec(shape, lambda b, f: (0, 0)),
        ),
        out_shape=jax.ShapeDtypeStruct(shape, jnp.float32),
        input_output_aliases=aliases,
        compiler_params=pltpu.CompilerParams(dimension_semantics=("arbitrary",)),
    )(*operands)


def combine(total):
    total = total.reshape(SPLITS, 4, ROWS * COLS)
    summed = (total[0] + total[1]) + total[2]
    return summed.reshape(4, NZ, CX, CY)


def shifted(block, axis, route_to):
    count = lax.axis_size(axis)
    return lax.ppermute(block, axis, [(i, (i + route_to) % count) for i in range(count)])


def bordered_density(density):
    head = density[:, :HALO, :]
    tail = density[:, CX - HALO :, :]
    wide = jnp.concatenate([density, shifted(head, "gx", -1), shifted(tail, "gx", 1)], axis=1)
    head = wide[:, :, :HALO]
    tail = wide[:, :, CY - HALO :]
    gap = jnp.zeros((NZ, WIDE_X, WIDE_Y - CY - 2 * HALO), jnp.float32)
    return jnp.concatenate([wide, shifted(head, "gy", -1), gap, shifted(tail, "gy", 1)], axis=2)


def near(v):
    flat = jnp.zeros((1,) + v.shape[1:], v.dtype)
    up = jnp.concatenate([v[1:], flat], axis=0)
    down = jnp.concatenate([flat, v[:-1]], axis=0)
    return (
        up
        + down
        + pltpu.roll(v, WIDE_X - 1, 1)
        + pltpu.roll(v, 1, 1)
        + pltpu.roll(v, WIDE_Y - 1, 2)
        + pltpu.roll(v, 1, 2)
    )


def relax_kernel(d_ref, o_ref):
    density = d_ref[...]
    source = COUPLING * ((density + SMOOTHING * (near(density) - 6.0 * density)) - BACKGROUND)
    shape = density.shape
    parity = (
        lax.broadcasted_iota(jnp.int32, shape, 0)
        + lax.broadcasted_iota(jnp.int32, shape, 1)
        + lax.broadcasted_iota(jnp.int32, shape, 2)
    ) % 2
    field = jnp.zeros(shape, jnp.float32)
    for sweep_no in range(SWEEPS):
        for colour in (0, 1):
            middle = field
            residual = (
                near(middle)
                - 6.0 * middle
                - SCREENING * middle
                - CUBIC_TERM * middle * middle * middle
                - source
            )
            slope = -6.0 - SCREENING - 3.0 * CUBIC_TERM * middle * middle
            field = jnp.where(parity == colour, middle - residual / slope, middle)
    o_ref[...] = field[:, :CX, :CY]


def relax(bordered):
    return pl.pallas_call(
        relax_kernel,
        out_shape=jax.ShapeDtypeStruct((NZ, CX, CY), jnp.float32),
    )(bordered)


def shards(payload, cells, counts):
    tallies = counts[0]
    limits = jnp.cumsum(tallies)
    starts = limits - tallies
    packed = jnp.concatenate([payload, cells.astype(jnp.float32)], axis=0)

    gx = lax.axis_size("gx")
    gy = lax.axis_size("gy")
    sends = []
    for which, (sx, sy) in enumerate(STEPS):
        capacity = CAP_F if which < 4 else CAP_D
        block = lax.dynamic_slice_in_dim(packed, starts[which], capacity, 1)
        living = (jnp.arange(capacity, dtype=jnp.int32) < tallies[which]).astype(jnp.float32)
        block = jnp.concatenate([block[0:1] * living[None, :], block[1:]], axis=0)
        route = []
        for ix in range(gx):
            for iy in range(gy):
                route.append((ix * gy + iy, ((ix + sx) % gx) * gy + (iy + sy) % gy))
        sends.append(lax.ppermute(block, ("gx", "gy"), route))

    total = deposit(payload, cells, starts[8].reshape(1))
    arrived = jnp.concatenate(sends, axis=1)
    total = deposit(arrived[0:4], arrived[4:7], jnp.zeros((1,), jnp.int32), total)
    interior = combine(total)
    density = interior[0]
    momentum = interior[1:]
    scalar_field = relax(bordered_density(density))
    return (scalar_field, momentum)


def solution(mesh):
    placed = (P(None, ("gx", "gy")), P(None, ("gx", "gy")), P(("gx", "gy"), None))
    return jax.shard_map(
        shards,
        mesh=mesh,
        in_specs=placed,
        out_specs=(P(None, "gx", "gy"), P(None, None, "gx", "gy")),
        check_vma=False,
    )
```

```python
import jax
import jax.numpy as jnp
from jax import lax
from jax.experimental import pallas as pl
from jax.experimental.pallas import tpu as pltpu
from jax.sharding import PartitionSpec as P

CX = 16
CY = 128
NZ = 8
SWEEPS = 4
PART = 16384
CAP_F = 2048
CAP_D = 512


SCREENING = 0.5
CUBIC_TERM = 0.3
COUPLING = 1.5
SMOOTHING = 0.1
BACKGROUND = 1.0

HALO = 2 * SWEEPS
ROWS = 64
COLS = 256
SPLITS = 3
BLOCK = 2048
LANE = 128
ARRIVED_BLOCK = (4 * CAP_F + 4 * CAP_D + 8 * LANE) // 4
WIDE_X = 2 * CX
WIDE_Y = 2 * CY

STEPS = ((1, 0), (-1, 0), (0, 1), (0, -1), (1, 1), (1, -1), (-1, 1), (-1, -1))


def local_start(count_ref):
    total = count_ref[0, 0]
    for edge in range(1, 8):
        total = total + count_ref[0, edge]
    return total


def no_start(count_ref):
    return 0


def deposit_body(first_of, block, first_ref, p_ref, c_ref, acc_ref, o_ref):
    step = pl.program_id(0)
    first = first_of(first_ref)

    @pl.when(step == 0)
    def _():
        if acc_ref is None:
            o_ref[...] = jnp.zeros(o_ref.shape, o_ref.dtype)
        else:
            o_ref[...] = acc_ref[...]

    @pl.when(step * block + block > first)
    def _():
        p = p_ref[...].astype(jnp.float32)
        c = c_ref[...].astype(jnp.int32)
        width = p.shape[1]
        masses = p[0:1]
        vals = jnp.concatenate([masses, masses * p[1:4]], axis=0)
        cell = (c[0:1] * CX + c[1:2]) * CY + c[2:3]
        position = step * block + lax.broadcasted_iota(jnp.int32, (1, width), 1)
        cell = jnp.where(position >= first, cell, -1)
        row = lax.shift_right_arithmetic(cell, 8)
        col = lax.bitwise_and(cell, COLS - 1)
        hi = vals.astype(jnp.bfloat16)
        rest = vals - hi.astype(jnp.float32)
        mid = rest.astype(jnp.bfloat16)
        lo = (rest - mid.astype(jnp.float32)).astype(jnp.bfloat16)
        parts = [q.astype(jnp.float32)[e : e + 1] for q in (hi, mid, lo) for e in range(4)]
        row_hot = (lax.broadcasted_iota(jnp.int32, (ROWS, width), 0) == row).astype(jnp.float32)
        left = jnp.concatenate([(row_hot * part).astype(jnp.bfloat16) for part in parts], axis=0)
        right = (lax.broadcasted_iota(jnp.int32, (COLS, width), 0) == col).astype(jnp.bfloat16)
        o_ref[...] += lax.dot_general(
            left, right, (((1,), (1,)), ((), ())), preferred_element_type=jnp.float32
        )


def deposit(values, targets, first, first_of, block, acc=None):
    count = values.shape[1] // block
    shape = (4 * SPLITS * ROWS, COLS)
    pick = lambda b, f: (0, jnp.maximum(b, first_of(f) // block))
    in_specs = [pl.BlockSpec((4, block), pick), pl.BlockSpec((3, block), pick)]
    operands = [first, values, targets]
    aliases = {}
    if acc is None:
        kernel = lambda f, p, c, o: deposit_body(first_of, block, f, p, c, None, o)
    else:
        kernel = lambda f, p, c, a, o: deposit_body(first_of, block, f, p, c, a, o)
        in_specs.append(pl.BlockSpec(shape, lambda b, f: (0, 0)))
        operands.append(acc)
        aliases = {3: 0}
    return pl.pallas_call(
        kernel,
        grid_spec=pltpu.PrefetchScalarGridSpec(
            num_scalar_prefetch=1,
            grid=(count,),
            in_specs=in_specs,
            out_specs=pl.BlockSpec(shape, lambda b, f: (0, 0)),
        ),
        out_shape=jax.ShapeDtypeStruct(shape, jnp.float32),
        input_output_aliases=aliases,
        compiler_params=pltpu.CompilerParams(dimension_semantics=("arbitrary",)),
    )(*operands)


def pack_kernel(count_ref, p_ref, c_ref, *out_refs):
    start = 0
    for which, out_ref in enumerate(out_refs):
        tally = count_ref[0, which]
        width = out_ref.shape[1]
        base = pl.multiple_of((start // LANE) * LANE, LANE)
        offset = start - base
        p = p_ref[:, pl.ds(base, width)]
        c = c_ref[:, pl.ds(base, width)]
        lane = lax.broadcasted_iota(jnp.int32, (1, width), 1)
        living = (lane >= offset) & (lane < offset + tally)
        out_ref[0:1, :] = jnp.where(living, p[0:1], 0.0)
        out_ref[1:4, :] = p[1:4]
        out_ref[4:7, :] = c.astype(jnp.float32)
        start = start + tally


def pack(payload, cells, counts):
    widths = [(CAP_F if which < 4 else CAP_D) + LANE for which in range(8)]
    return pl.pallas_call(
        pack_kernel,
        in_specs=[
            pl.BlockSpec(memory_space=pltpu.SMEM),
            pl.BlockSpec(memory_space=pltpu.VMEM),
            pl.BlockSpec(memory_space=pltpu.VMEM),
        ],
        out_shape=[jax.ShapeDtypeStruct((7, w), jnp.float32) for w in widths],
    )(counts, payload, cells)


def combine(total):
    total = total.reshape(SPLITS, 4, ROWS * COLS)
    summed = (total[0] + total[1]) + total[2]
    return summed.reshape(4, NZ, CX, CY)


def towards(block, sx, sy):
    gx = lax.axis_size("gx")
    gy = lax.axis_size("gy")
    route = []
    for ix in range(gx):
        for iy in range(gy):
            route.append((ix * gy + iy, ((ix + sx) % gx) * gy + (iy + sy) % gy))
    return lax.ppermute(block, ("gx", "gy"), route)


def bordered_density(density):
    low_x, high_x = slice(0, HALO), slice(CX - HALO, CX)
    low_y, high_y = slice(0, HALO), slice(CY - HALO, CY)
    every = slice(None)
    upper_x = towards(density[:, low_x, :], -1, 0)
    lower_x = towards(density[:, high_x, :], 1, 0)
    upper_y = towards(density[:, :, low_y], 0, -1)
    lower_y = towards(density[:, :, high_y], 0, 1)
    upper_both = towards(density[:, low_x, low_y], -1, -1)
    upper_lower = towards(density[:, low_x, high_y], -1, 1)
    lower_upper = towards(density[:, high_x, low_y], 1, -1)
    lower_both = towards(density[:, high_x, high_y], 1, 1)
    wide = jnp.concatenate([density, upper_x, lower_x], axis=1)
    right = jnp.concatenate([upper_y, upper_both, lower_upper], axis=1)
    left = jnp.concatenate([lower_y, upper_lower, lower_both], axis=1)
    gap = jnp.zeros((NZ, WIDE_X, WIDE_Y - CY - 2 * HALO), jnp.float32)
    return jnp.concatenate([wide, right, gap, left], axis=2)


def near(v):
    flat = jnp.zeros((1,) + v.shape[1:], v.dtype)
    up = jnp.concatenate([v[1:], flat], axis=0)
    down = jnp.concatenate([flat, v[:-1]], axis=0)
    return (
        up
        + down
        + pltpu.roll(v, WIDE_X - 1, 1)
        + pltpu.roll(v, 1, 1)
        + pltpu.roll(v, WIDE_Y - 1, 2)
        + pltpu.roll(v, 1, 2)
    )


def relax_kernel(d_ref, o_ref):
    density = d_ref[...]
    source = COUPLING * ((density + SMOOTHING * (near(density) - 6.0 * density)) - BACKGROUND)
    shape = density.shape
    parity = (
        lax.broadcasted_iota(jnp.int32, shape, 0)
        + lax.broadcasted_iota(jnp.int32, shape, 1)
        + lax.broadcasted_iota(jnp.int32, shape, 2)
    ) % 2
    field = jnp.zeros(shape, jnp.float32)
    for sweep_no in range(SWEEPS):
        for colour in (0, 1):
            middle = field
            residual = (
                near(middle)
                - 6.0 * middle
                - SCREENING * middle
                - CUBIC_TERM * middle * middle * middle
                - source
            )
            slope = -6.0 - SCREENING - 3.0 * CUBIC_TERM * middle * middle
            field = jnp.where(parity == colour, middle - residual / slope, middle)
    o_ref[...] = field[:, :CX, :CY]


def relax(bordered):
    return pl.pallas_call(
        relax_kernel,
        out_shape=jax.ShapeDtypeStruct((NZ, CX, CY), jnp.float32),
    )(bordered)


def shards(payload, cells, counts):
    blocks = pack(payload, cells, counts)
    sends = [towards(block, sx, sy) for block, (sx, sy) in zip(blocks, STEPS)]
    total = deposit(payload, cells, counts, local_start, BLOCK)
    arrived = jnp.concatenate(sends, axis=1)
    total = deposit(arrived[0:4], arrived[4:7], counts, no_start, ARRIVED_BLOCK, total)
    interior = combine(total)
    density = interior[0]
    momentum = interior[1:]
    scalar_field = relax(bordered_density(density))
    return (scalar_field, momentum)


def solution(mesh):
    placed = (P(None, ("gx", "gy")), P(None, ("gx", "gy")), P(("gx", "gy"), None))
    return jax.shard_map(
        shards,
        mesh=mesh,
        in_specs=placed,
        out_specs=(P(None, "gx", "gy"), P(None, None, "gx", "gy")),
        check_vma=False,
    )
```

```python
import jax
import jax.numpy as jnp
from jax import lax
from jax.experimental import pallas as pl
from jax.experimental.pallas import tpu as pltpu
from jax.sharding import PartitionSpec as P

CX = 16
CY = 128
NZ = 8
SWEEPS = 4
PART = 16384
CAP_F = 2048
CAP_D = 512


SCREENING = 0.5
CUBIC_TERM = 0.3
COUPLING = 1.5
SMOOTHING = 0.1
BACKGROUND = 1.0

HALO = 2 * SWEEPS
ROWS = 64
COLS = 256
SPLITS = 3
BLOCK = 2048
LANE = 128
ARRIVED_BLOCK = (4 * CAP_F + 4 * CAP_D + 8 * LANE) // 4
WIDE_X = 2 * CX
WIDE_Y = 2 * CY

STEPS = ((1, 0), (-1, 0), (0, 1), (0, -1), (1, 1), (1, -1), (-1, 1), (-1, -1))


def local_start(count_ref):
    total = count_ref[0, 0]
    for edge in range(1, 8):
        total = total + count_ref[0, edge]
    return total


def accumulate(first, block, step, p, c, acc_ref):
    width = p.shape[1]
    masses = p[0:1]
    vals = jnp.concatenate([masses, masses * p[1:4]], axis=0)
    cell = (c[0:1] * CX + c[1:2]) * CY + c[2:3]
    position = step * block + lax.broadcasted_iota(jnp.int32, (1, width), 1)
    cell = jnp.where(position >= first, cell, -1)
    row = lax.shift_right_arithmetic(cell, 8)
    col = lax.bitwise_and(cell, COLS - 1)
    hi = vals.astype(jnp.bfloat16)
    rest = vals - hi.astype(jnp.float32)
    mid = rest.astype(jnp.bfloat16)
    lo = (rest - mid.astype(jnp.float32)).astype(jnp.bfloat16)
    parts = [q.astype(jnp.float32)[e : e + 1] for q in (hi, mid, lo) for e in range(4)]
    row_hot = (lax.broadcasted_iota(jnp.int32, (ROWS, width), 0) == row).astype(jnp.float32)
    left = jnp.concatenate([(row_hot * part).astype(jnp.bfloat16) for part in parts], axis=0)
    right = (lax.broadcasted_iota(jnp.int32, (COLS, width), 0) == col).astype(jnp.bfloat16)
    acc_ref[...] += lax.dot_general(
        left, right, (((1,), (1,)), ((), ())), preferred_element_type=jnp.float32
    )


def local_kernel(count_ref, p_ref, c_ref, o_ref):
    step = pl.program_id(0)
    first = local_start(count_ref)

    @pl.when(step == 0)
    def _():
        o_ref[...] = jnp.zeros(o_ref.shape, o_ref.dtype)

    @pl.when(step * BLOCK + BLOCK > first)
    def _():
        accumulate(first, BLOCK, step, p_ref[...], c_ref[...], o_ref)


def arrived_kernel(x_ref, a_ref, o_ref):
    step = pl.program_id(0)

    @pl.when(step == 0)
    def _():
        o_ref[...] = a_ref[...]

    x = x_ref[...]
    accumulate(0, ARRIVED_BLOCK, step, x[0:4], x[4:7].astype(jnp.int32), o_ref)


ACC_SHAPE = (4 * SPLITS * ROWS, COLS)


def deposit_local(payload, cells, counts):
    pick = lambda b, f: (0, jnp.maximum(b, local_start(f) // BLOCK))
    return pl.pallas_call(
        local_kernel,
        grid_spec=pltpu.PrefetchScalarGridSpec(
            num_scalar_prefetch=1,
            grid=(payload.shape[1] // BLOCK,),
            in_specs=[pl.BlockSpec((4, BLOCK), pick), pl.BlockSpec((3, BLOCK), pick)],
            out_specs=pl.BlockSpec(ACC_SHAPE, lambda b, f: (0, 0)),
        ),
        out_shape=jax.ShapeDtypeStruct(ACC_SHAPE, jnp.float32),
        compiler_params=pltpu.CompilerParams(dimension_semantics=("arbitrary",)),
    )(counts, payload, cells)


def deposit_arrived(arrived, acc):
    shape = ACC_SHAPE
    return pl.pallas_call(
        arrived_kernel,
        grid=(arrived.shape[1] // ARRIVED_BLOCK,),
        in_specs=[
            pl.BlockSpec((7, ARRIVED_BLOCK), lambda b: (0, b)),
            pl.BlockSpec(ACC_SHAPE, lambda b: (0, 0)),
        ],
        out_specs=pl.BlockSpec(shape, lambda b: (0, 0)),
        out_shape=jax.ShapeDtypeStruct(shape, jnp.float32),
        input_output_aliases={1: 0},
        compiler_params=pltpu.CompilerParams(dimension_semantics=("arbitrary",)),
    )(arrived, acc)


def pack_kernel(count_ref, p_ref, c_ref, *out_refs):
    start = 0
    for which, out_ref in enumerate(out_refs):
        tally = count_ref[0, which]
        width = out_ref.shape[1]
        base = pl.multiple_of((start // LANE) * LANE, LANE)
        offset = start - base
        p = p_ref[:, pl.ds(base, width)]
        c = c_ref[:, pl.ds(base, width)]
        lane = lax.broadcasted_iota(jnp.int32, (1, width), 1)
        living = (lane >= offset) & (lane < offset + tally)
        out_ref[0:1, :] = jnp.where(living, p[0:1], 0.0)
        out_ref[1:4, :] = p[1:4]
        out_ref[4:7, :] = c.astype(jnp.float32)
        start = start + tally


def pack(payload, cells, counts):
    widths = [(CAP_F if which < 4 else CAP_D) + LANE for which in range(8)]
    return pl.pallas_call(
        pack_kernel,
        in_specs=[
            pl.BlockSpec(memory_space=pltpu.SMEM),
            pl.BlockSpec(memory_space=pltpu.VMEM),
            pl.BlockSpec(memory_space=pltpu.VMEM),
        ],
        out_shape=[jax.ShapeDtypeStruct((7, w), jnp.float32) for w in widths],
    )(counts, payload, cells)


def towards(block, sx, sy):
    gx = lax.axis_size("gx")
    gy = lax.axis_size("gy")
    route = []
    for ix in range(gx):
        for iy in range(gy):
            route.append((ix * gy + iy, ((ix + sx) % gx) * gy + (iy + sy) % gy))
    return lax.ppermute(block, ("gx", "gy"), route)


def bordered_density(density):
    low_x, high_x = slice(0, HALO), slice(CX - HALO, CX)
    low_y, high_y = slice(0, HALO), slice(CY - HALO, CY)
    every = slice(None)
    upper_x = towards(density[:, low_x, :], -1, 0)
    lower_x = towards(density[:, high_x, :], 1, 0)
    upper_y = towards(density[:, :, low_y], 0, -1)
    lower_y = towards(density[:, :, high_y], 0, 1)
    upper_both = towards(density[:, low_x, low_y], -1, -1)
    upper_lower = towards(density[:, low_x, high_y], -1, 1)
    lower_upper = towards(density[:, high_x, low_y], 1, -1)
    lower_both = towards(density[:, high_x, high_y], 1, 1)
    wide = jnp.concatenate([density, upper_x, lower_x], axis=1)
    right = jnp.concatenate([upper_y, upper_both, lower_upper], axis=1)
    left = jnp.concatenate([lower_y, upper_lower, lower_both], axis=1)
    gap = jnp.zeros((NZ, WIDE_X, WIDE_Y - CY - 2 * HALO), jnp.float32)
    return jnp.concatenate([wide, right, gap, left], axis=2)


def near(v):
    flat = jnp.zeros((1,) + v.shape[1:], v.dtype)
    up = jnp.concatenate([v[1:], flat], axis=0)
    down = jnp.concatenate([flat, v[:-1]], axis=0)
    return (
        up
        + down
        + pltpu.roll(v, WIDE_X - 1, 1)
        + pltpu.roll(v, 1, 1)
        + pltpu.roll(v, WIDE_Y - 1, 2)
        + pltpu.roll(v, 1, 2)
    )


def relax_kernel(d_ref, o_ref):
    density = d_ref[...]
    source = COUPLING * ((density + SMOOTHING * (near(density) - 6.0 * density)) - BACKGROUND)
    shape = density.shape
    parity = (
        lax.broadcasted_iota(jnp.int32, shape, 0)
        + lax.broadcasted_iota(jnp.int32, shape, 1)
        + lax.broadcasted_iota(jnp.int32, shape, 2)
    ) % 2
    field = jnp.zeros(shape, jnp.float32)
    for sweep_no in range(SWEEPS):
        for colour in (0, 1):
            middle = field
            residual = (
                near(middle)
                - 6.0 * middle
                - SCREENING * middle
                - CUBIC_TERM * middle * middle * middle
                - source
            )
            slope = -6.0 - SCREENING - 3.0 * CUBIC_TERM * middle * middle
            field = jnp.where(parity == colour, middle - residual / slope, middle)
    o_ref[...] = field[:, :CX, :CY]


def relax(bordered):
    return pl.pallas_call(
        relax_kernel,
        out_shape=jax.ShapeDtypeStruct((NZ, CX, CY), jnp.float32),
    )(bordered)


def shards(payload, cells, counts):
    blocks = pack(payload, cells, counts)
    sends = [towards(block, sx, sy) for block, (sx, sy) in zip(blocks, STEPS)]
    total = deposit_local(payload, cells, counts)
    arrived = jnp.concatenate(sends, axis=1)
    total = deposit_arrived(arrived, total).reshape(SPLITS, 4, ROWS * COLS)
    interior = ((total[0] + total[1]) + total[2]).reshape(4, NZ, CX, CY)
    density = interior[0]
    momentum = interior[1:]
    scalar_field = relax(bordered_density(density))
    return (scalar_field, momentum)


def solution(mesh):
    placed = (P(None, ("gx", "gy")), P(None, ("gx", "gy")), P(("gx", "gy"), None))
    return jax.shard_map(
        shards,
        mesh=mesh,
        in_specs=placed,
        out_specs=(P(None, "gx", "gy"), P(None, None, "gx", "gy")),
        check_vma=False,
    )
```

```python
import jax
import jax.numpy as jnp
from jax import lax
from jax.experimental import pallas as pl
from jax.experimental.pallas import tpu as pltpu
from jax.sharding import PartitionSpec as P

CX = 16
CY = 128
NZ = 8
SWEEPS = 4
PART = 16384
CAP_F = 2048
CAP_D = 512


SCREENING = 0.5
CUBIC_TERM = 0.3
COUPLING = 1.5
SMOOTHING = 0.1
BACKGROUND = 1.0

HALO = 2 * SWEEPS
ROWS = 64
COLS = 256
SPLITS = 3
BLOCK = 2048
LANE = 128
ARRIVED_BLOCK = (4 * CAP_F + 4 * CAP_D + 8 * LANE) // 4
WIDE_X = 2 * CX
WIDE_Y = 2 * CY

STEPS = ((1, 0), (-1, 0), (0, 1), (0, -1), (1, 1), (1, -1), (-1, 1), (-1, -1))


def local_start(count_ref):
    total = count_ref[0, 0]
    for edge in range(1, 8):
        total = total + count_ref[0, edge]
    return total


def accumulate(first, block, step, p, c, acc_ref):
    width = p.shape[1]
    masses = p[0:1]
    vals = jnp.concatenate([masses, masses * p[1:4]], axis=0)
    cell = (c[0:1] * CX + c[1:2]) * CY + c[2:3]
    position = step * block + lax.broadcasted_iota(jnp.int32, (1, width), 1)
    cell = jnp.where(position >= first, cell, -1)
    row = lax.shift_right_arithmetic(cell, 8)
    col = lax.bitwise_and(cell, COLS - 1)
    hi = vals.astype(jnp.bfloat16)
    rest = vals - hi.astype(jnp.float32)
    mid = rest.astype(jnp.bfloat16)
    lo = (rest - mid.astype(jnp.float32)).astype(jnp.bfloat16)
    parts = [q.astype(jnp.float32)[e : e + 1] for q in (hi, mid, lo) for e in range(4)]
    row_hot = (lax.broadcasted_iota(jnp.int32, (ROWS, width), 0) == row).astype(jnp.float32)
    left = jnp.concatenate([(row_hot * part).astype(jnp.bfloat16) for part in parts], axis=0)
    right = (lax.broadcasted_iota(jnp.int32, (COLS, width), 0) == col).astype(jnp.bfloat16)
    acc_ref[...] += lax.dot_general(
        left, right, (((1,), (1,)), ((), ())), preferred_element_type=jnp.float32
    )


def local_kernel(count_ref, p_ref, c_ref, o_ref):
    step = pl.program_id(0)
    first = local_start(count_ref)

    @pl.when(step == 0)
    def _():
        o_ref[...] = jnp.zeros(o_ref.shape, o_ref.dtype)

    @pl.when(step * BLOCK + BLOCK > first)
    def _():
        accumulate(first, BLOCK, step, p_ref[...], c_ref[...], o_ref)


def arrived_kernel(block, x_ref, a_ref, o_ref):
    step = pl.program_id(0)

    @pl.when(step == 0)
    def _():
        o_ref[...] = a_ref[...]

    x = x_ref[...]
    accumulate(0, block, step, x[0:4], x[4:7].astype(jnp.int32), o_ref)


ACC_SHAPE = (4 * SPLITS * ROWS, COLS)


def deposit_local(payload, cells, counts):
    pick = lambda b, f: (0, jnp.maximum(b, local_start(f) // BLOCK))
    return pl.pallas_call(
        local_kernel,
        grid_spec=pltpu.PrefetchScalarGridSpec(
            num_scalar_prefetch=1,
            grid=(payload.shape[1] // BLOCK,),
            in_specs=[pl.BlockSpec((4, BLOCK), pick), pl.BlockSpec((3, BLOCK), pick)],
            out_specs=pl.BlockSpec(ACC_SHAPE, lambda b, f: (0, 0)),
        ),
        out_shape=jax.ShapeDtypeStruct(ACC_SHAPE, jnp.float32),
        compiler_params=pltpu.CompilerParams(dimension_semantics=("arbitrary",)),
    )(counts, payload, cells)


def deposit_arrived(arrived, acc, block):
    shape = ACC_SHAPE
    return pl.pallas_call(
        lambda x, a, o: arrived_kernel(block, x, a, o),
        grid=(arrived.shape[1] // block,),
        in_specs=[
            pl.BlockSpec((7, block), lambda b: (0, b)),
            pl.BlockSpec(ACC_SHAPE, lambda b: (0, 0)),
        ],
        out_specs=pl.BlockSpec(shape, lambda b: (0, 0)),
        out_shape=jax.ShapeDtypeStruct(shape, jnp.float32),
        input_output_aliases={1: 0},
        compiler_params=pltpu.CompilerParams(dimension_semantics=("arbitrary",)),
    )(arrived, acc)


def pack_kernel(count_ref, p_ref, c_ref, plus_x, minus_x, plus_y, minus_y):
    face = CAP_F + LANE
    corner = CAP_D + LANE
    places = (
        (plus_x, 0), (minus_x, 0), (plus_y, 0), (minus_y, 0),
        (plus_x, face), (plus_x, face + corner), (minus_x, face), (minus_x, face + corner),
    )
    start = 0
    for which, (out_ref, column) in enumerate(places):
        tally = count_ref[0, which]
        width = face if which < 4 else corner
        base = pl.multiple_of((start // LANE) * LANE, LANE)
        offset = start - base
        p = p_ref[:, pl.ds(base, width)]
        c = c_ref[:, pl.ds(base, width)]
        lane = lax.broadcasted_iota(jnp.int32, (1, width), 1)
        living = (lane >= offset) & (lane < offset + tally)
        out_ref[0:1, column : column + width] = jnp.where(living, p[0:1], 0.0)
        out_ref[1:4, column : column + width] = p[1:4]
        out_ref[4:7, column : column + width] = c.astype(jnp.float32)
        start = start + tally


def pack(payload, cells, counts):
    face = CAP_F + LANE
    corner = CAP_D + LANE
    widths = (face + 2 * corner, face + 2 * corner, face, face)
    return pl.pallas_call(
        pack_kernel,
        in_specs=[
            pl.BlockSpec(memory_space=pltpu.SMEM),
            pl.BlockSpec(memory_space=pltpu.VMEM),
            pl.BlockSpec(memory_space=pltpu.VMEM),
        ],
        out_shape=[jax.ShapeDtypeStruct((7, w), jnp.float32) for w in widths],
    )(counts, payload, cells)


def towards(block, sx, sy):
    gx = lax.axis_size("gx")
    gy = lax.axis_size("gy")
    route = []
    for ix in range(gx):
        for iy in range(gy):
            route.append((ix * gy + iy, ((ix + sx) % gx) * gy + (iy + sy) % gy))
    return lax.ppermute(block, ("gx", "gy"), route)


def bordered_density(density):
    upper_x = towards(density[:, :HALO, :], -1, 0)
    lower_x = towards(density[:, CX - HALO :, :], 1, 0)
    wide = jnp.concatenate([density, upper_x, lower_x], axis=1)
    upper_y = towards(wide[:, :, :HALO], 0, -1)
    lower_y = towards(wide[:, :, CY - HALO :], 0, 1)
    gap = jnp.zeros((NZ, WIDE_X, WIDE_Y - CY - 2 * HALO), jnp.float32)
    return jnp.concatenate([wide, upper_y, gap, lower_y], axis=2)


def near(v):
    flat = jnp.zeros((1,) + v.shape[1:], v.dtype)
    up = jnp.concatenate([v[1:], flat], axis=0)
    down = jnp.concatenate([flat, v[:-1]], axis=0)
    return (
        up
        + down
        + pltpu.roll(v, WIDE_X - 1, 1)
        + pltpu.roll(v, 1, 1)
        + pltpu.roll(v, WIDE_Y - 1, 2)
        + pltpu.roll(v, 1, 2)
    )


def relax_kernel(d_ref, o_ref):
    density = d_ref[...]
    source = COUPLING * ((density + SMOOTHING * (near(density) - 6.0 * density)) - BACKGROUND)
    shape = density.shape
    parity = (
        lax.broadcasted_iota(jnp.int32, shape, 0)
        + lax.broadcasted_iota(jnp.int32, shape, 1)
        + lax.broadcasted_iota(jnp.int32, shape, 2)
    ) % 2
    field = jnp.zeros(shape, jnp.float32)
    for sweep_no in range(SWEEPS):
        for colour in (0, 1):
            middle = field
            residual = (
                near(middle)
                - 6.0 * middle
                - SCREENING * middle
                - CUBIC_TERM * middle * middle * middle
                - source
            )
            slope = -6.0 - SCREENING - 3.0 * CUBIC_TERM * middle * middle
            field = jnp.where(parity == colour, middle - residual / slope, middle)
    o_ref[...] = field[:, :CX, :CY]


def relax(bordered):
    return pl.pallas_call(
        relax_kernel,
        out_shape=jax.ShapeDtypeStruct((NZ, CX, CY), jnp.float32),
    )(bordered)


def shards(payload, cells, counts):
    face = CAP_F + LANE
    corner = CAP_D + LANE
    plus_x, minus_x, plus_y, minus_y = pack(payload, cells, counts)
    from_minus_x = towards(plus_x, 1, 0)
    from_plus_x = towards(minus_x, -1, 0)
    total = deposit_local(payload, cells, counts)
    plus_y = jnp.concatenate(
        [plus_y, from_minus_x[:, face : face + corner], from_plus_x[:, face : face + corner]], axis=1
    )
    minus_y = jnp.concatenate(
        [minus_y, from_minus_x[:, face + corner :], from_plus_x[:, face + corner :]], axis=1
    )
    from_minus_y = towards(plus_y, 0, 1)
    from_plus_y = towards(minus_y, 0, -1)
    faces = jnp.concatenate([from_minus_x[:, :face], from_plus_x[:, :face]], axis=1)
    total = deposit_arrived(faces, total, face)
    crossing = jnp.concatenate([from_minus_y, from_plus_y], axis=1)
    total = deposit_arrived(crossing, total, face + 2 * corner)
    total = total.reshape(SPLITS, 4, ROWS * COLS)
    interior = ((total[0] + total[1]) + total[2]).reshape(4, NZ, CX, CY)
    density = interior[0]
    momentum = interior[1:]
    scalar_field = relax(bordered_density(density))
    return (scalar_field, momentum)


def solution(mesh):
    placed = (P(None, ("gx", "gy")), P(None, ("gx", "gy")), P(("gx", "gy"), None))
    return jax.shard_map(
        shards,
        mesh=mesh,
        in_specs=placed,
        out_specs=(P(None, "gx", "gy"), P(None, None, "gx", "gy")),
        check_vma=False,
    )
```

```python
import jax
import jax.numpy as jnp
from jax import lax
from jax.experimental import pallas as pl
from jax.experimental.pallas import tpu as pltpu
from jax.sharding import PartitionSpec as P

CX = 16
CY = 128
NZ = 8
SWEEPS = 4
PART = 16384
CAP_F = 2048
CAP_D = 512


SCREENING = 0.5
CUBIC_TERM = 0.3
COUPLING = 1.5
SMOOTHING = 0.1
BACKGROUND = 1.0

HALO = 2 * SWEEPS
ROWS = 64
COLS = 256
SPLITS = 2
BLOCK = 2048
LANE = 128
WIDE_X = 2 * CX
WIDE_Y = 2 * CY

STEPS = ((1, 0), (-1, 0), (0, 1), (0, -1), (1, 1), (1, -1), (-1, 1), (-1, -1))


def local_start(count_ref):
    total = count_ref[0, 0]
    for edge in range(1, 8):
        total = total + count_ref[0, edge]
    return total


def accumulate(first, block, step, p, c, acc_ref):
    width = p.shape[1]
    masses = p[0:1]
    vals = jnp.concatenate([masses, masses * p[1:4]], axis=0)
    cell = (c[0:1] * CX + c[1:2]) * CY + c[2:3]
    position = step * block + lax.broadcasted_iota(jnp.int32, (1, width), 1)
    cell = jnp.where(position >= first, cell, -1)
    row = lax.shift_right_arithmetic(cell, 8)
    col = lax.bitwise_and(cell, COLS - 1)
    hi = vals.astype(jnp.bfloat16)
    lo = (vals - hi.astype(jnp.float32)).astype(jnp.bfloat16)
    parts = [q.astype(jnp.float32)[e : e + 1] for q in (hi, lo) for e in range(4)]
    row_hot = (lax.broadcasted_iota(jnp.int32, (ROWS, width), 0) == row).astype(jnp.float32)
    left = jnp.concatenate([(row_hot * part).astype(jnp.bfloat16) for part in parts], axis=0)
    right = (lax.broadcasted_iota(jnp.int32, (COLS, width), 0) == col).astype(jnp.bfloat16)
    acc_ref[...] += lax.dot_general(
        left, right, (((1,), (1,)), ((), ())), preferred_element_type=jnp.float32
    )


def local_kernel(count_ref, p_ref, c_ref, o_ref):
    step = pl.program_id(0)
    first = local_start(count_ref)

    @pl.when(step == 0)
    def _():
        o_ref[...] = jnp.zeros(o_ref.shape, o_ref.dtype)

    @pl.when(step * BLOCK + BLOCK > first)
    def _():
        accumulate(first, BLOCK, step, p_ref[...], c_ref[...], o_ref)


def arrived_kernel(block, x_ref, y_ref, a_ref, o_ref):
    o_ref[...] = a_ref[...]
    for source in (x_ref, y_ref):
        x = source[...]
        accumulate(0, block, 0, x[0:4], x[4:7].astype(jnp.int32), o_ref)


ACC_SHAPE = (4 * SPLITS * ROWS, COLS)


def deposit_local(payload, cells, counts):
    pick = lambda b, f: (0, jnp.maximum(b, local_start(f) // BLOCK))
    return pl.pallas_call(
        local_kernel,
        grid_spec=pltpu.PrefetchScalarGridSpec(
            num_scalar_prefetch=1,
            grid=(payload.shape[1] // BLOCK,),
            in_specs=[pl.BlockSpec((4, BLOCK), pick), pl.BlockSpec((3, BLOCK), pick)],
            out_specs=pl.BlockSpec(ACC_SHAPE, lambda b, f: (0, 0)),
        ),
        out_shape=jax.ShapeDtypeStruct(ACC_SHAPE, jnp.float32),
        compiler_params=pltpu.CompilerParams(dimension_semantics=("arbitrary",)),
    )(counts, payload, cells)


def deposit_arrived(first, second, acc, block):
    return pl.pallas_call(
        lambda x, y, a, o: arrived_kernel(block, x, y, a, o),
        grid=(1,),
        in_specs=[
            pl.BlockSpec((7, block), lambda b: (0, 0)),
            pl.BlockSpec((7, block), lambda b: (0, 0)),
            pl.BlockSpec(ACC_SHAPE, lambda b: (0, 0)),
        ],
        out_specs=pl.BlockSpec(ACC_SHAPE, lambda b: (0, 0)),
        out_shape=jax.ShapeDtypeStruct(ACC_SHAPE, jnp.float32),
        input_output_aliases={2: 0},
    )(first, second, acc)


def pack_kernel(count_ref, p_ref, c_ref, plus_x, minus_x, plus_y, minus_y):
    face = CAP_F + LANE
    corner = CAP_D + LANE
    places = (
        (plus_x, 0), (minus_x, 0), (plus_y, 0), (minus_y, 0),
        (plus_x, face), (plus_x, face + corner), (minus_x, face), (minus_x, face + corner),
    )
    start = 0
    for which, (out_ref, column) in enumerate(places):
        tally = count_ref[0, which]
        width = face if which < 4 else corner
        base = pl.multiple_of((start // LANE) * LANE, LANE)
        offset = start - base
        p = p_ref[:, pl.ds(base, width)]
        c = c_ref[:, pl.ds(base, width)]
        lane = lax.broadcasted_iota(jnp.int32, (1, width), 1)
        living = (lane >= offset) & (lane < offset + tally)
        out_ref[0:1, column : column + width] = jnp.where(living, p[0:1], 0.0)
        out_ref[1:4, column : column + width] = p[1:4]
        out_ref[4:7, column : column + width] = c.astype(jnp.float32)
        start = start + tally


def pack(payload, cells, counts):
    face = CAP_F + LANE
    corner = CAP_D + LANE
    widths = (face + 2 * corner, face + 2 * corner, face, face)
    return pl.pallas_call(
        pack_kernel,
        in_specs=[
            pl.BlockSpec(memory_space=pltpu.SMEM),
            pl.BlockSpec(memory_space=pltpu.VMEM),
            pl.BlockSpec(memory_space=pltpu.VMEM),
        ],
        out_shape=[jax.ShapeDtypeStruct((7, w), jnp.float32) for w in widths],
    )(counts, payload, cells)


def towards(block, sx, sy):
    gx = lax.axis_size("gx")
    gy = lax.axis_size("gy")
    route = []
    for ix in range(gx):
        for iy in range(gy):
            route.append((ix * gy + iy, ((ix + sx) % gx) * gy + (iy + sy) % gy))
    return lax.ppermute(block, ("gx", "gy"), route)


def bordered_density(density):
    upper_x = towards(density[:, :HALO, :], -1, 0)
    lower_x = towards(density[:, CX - HALO :, :], 1, 0)
    wide = jnp.concatenate([density, upper_x, lower_x], axis=1)
    upper_y = towards(wide[:, :, :HALO], 0, -1)
    lower_y = towards(wide[:, :, CY - HALO :], 0, 1)
    gap = jnp.zeros((NZ, WIDE_X, WIDE_Y - CY - 2 * HALO), jnp.float32)
    return jnp.concatenate([wide, upper_y, gap, lower_y], axis=2)


def near(v):
    flat = jnp.zeros((1,) + v.shape[1:], v.dtype)
    up = jnp.concatenate([v[1:], flat], axis=0)
    down = jnp.concatenate([flat, v[:-1]], axis=0)
    return (
        up
        + down
        + pltpu.roll(v, WIDE_X - 1, 1)
        + pltpu.roll(v, 1, 1)
        + pltpu.roll(v, WIDE_Y - 1, 2)
        + pltpu.roll(v, 1, 2)
    )


def relax_kernel(d_ref, o_ref):
    density = d_ref[...]
    source = COUPLING * ((density + SMOOTHING * (near(density) - 6.0 * density)) - BACKGROUND)
    shape = density.shape
    parity = (
        lax.broadcasted_iota(jnp.int32, shape, 0)
        + lax.broadcasted_iota(jnp.int32, shape, 1)
        + lax.broadcasted_iota(jnp.int32, shape, 2)
    ) % 2
    field = jnp.zeros(shape, jnp.float32)
    for sweep_no in range(SWEEPS):
        for colour in (0, 1):
            middle = field
            residual = (
                near(middle)
                - 6.0 * middle
                - SCREENING * middle
                - CUBIC_TERM * middle * middle * middle
                - source
            )
            slope = -6.0 - SCREENING - 3.0 * CUBIC_TERM * middle * middle
            field = jnp.where(parity == colour, middle - residual / slope, middle)
    o_ref[...] = field[:, :CX, :CY]


def relax(bordered):
    return pl.pallas_call(
        relax_kernel,
        out_shape=jax.ShapeDtypeStruct((NZ, CX, CY), jnp.float32),
    )(bordered)


def shards(payload, cells, counts):
    face = CAP_F + LANE
    corner = CAP_D + LANE
    plus_x, minus_x, plus_y, minus_y = pack(payload, cells, counts)
    from_minus_x = towards(plus_x, 1, 0)
    from_plus_x = towards(minus_x, -1, 0)
    total = deposit_local(payload, cells, counts)
    plus_y = jnp.concatenate(
        [plus_y, from_minus_x[:, face : face + corner], from_plus_x[:, face : face + corner]], axis=1
    )
    minus_y = jnp.concatenate(
        [minus_y, from_minus_x[:, face + corner :], from_plus_x[:, face + corner :]], axis=1
    )
    from_minus_y = towards(plus_y, 0, 1)
    from_plus_y = towards(minus_y, 0, -1)
    total = deposit_arrived(from_minus_x, from_plus_x, total, face)
    total = deposit_arrived(from_minus_y, from_plus_y, total, face + 2 * corner)
    total = total.reshape(SPLITS, 4, ROWS * COLS)
    interior = (total[0] + total[1]).reshape(4, NZ, CX, CY)
    density = interior[0]
    momentum = interior[1:]
    scalar_field = relax(bordered_density(density))
    return (scalar_field, momentum)


def solution(mesh):
    placed = (P(None, ("gx", "gy")), P(None, ("gx", "gy")), P(("gx", "gy"), None))
    return jax.shard_map(
        shards,
        mesh=mesh,
        in_specs=placed,
        out_specs=(P(None, "gx", "gy"), P(None, None, "gx", "gy")),
        check_vma=False,
    )
```

```python
import jax
import jax.numpy as jnp
from jax import lax
from jax.experimental import pallas as pl
from jax.experimental.pallas import tpu as pltpu
from jax.sharding import PartitionSpec as P

CX = 16
CY = 128
NZ = 8
SWEEPS = 4
CAP_F = 2048
CAP_D = 512


SCREENING = 0.5
CUBIC_TERM = 0.3
COUPLING = 1.5
SMOOTHING = 0.1
BACKGROUND = 1.0

HALO = 2 * SWEEPS
ROWS = 64
COLS = 256
SPLITS = 2
BLOCK = 2048
LANE = 128
WIDE_X = 2 * CX
WIDE_Y = 2 * CY


def local_start(count_ref):
    total = count_ref[0, 0]
    for edge in range(1, 8):
        total = total + count_ref[0, edge]
    return total


def accumulate(first, block, step, p, c, acc_ref):
    width = p.shape[1]
    masses = p[0:1]
    vals = jnp.concatenate([masses, masses * p[1:4]], axis=0)
    cell = (c[0:1] * CX + c[1:2]) * CY + c[2:3]
    position = step * block + lax.broadcasted_iota(jnp.int32, (1, width), 1)
    cell = jnp.where(position >= first, cell, -1)
    row = lax.shift_right_arithmetic(cell, 8)
    col = lax.bitwise_and(cell, COLS - 1)
    hi = vals.astype(jnp.bfloat16)
    lo = (vals - hi.astype(jnp.float32)).astype(jnp.bfloat16)
    parts = [q.astype(jnp.float32)[e : e + 1] for q in (hi, lo) for e in range(4)]
    row_hot = (lax.broadcasted_iota(jnp.int32, (ROWS, width), 0) == row).astype(jnp.float32)
    left = jnp.concatenate([(row_hot * part).astype(jnp.bfloat16) for part in parts], axis=0)
    right = (lax.broadcasted_iota(jnp.int32, (COLS, width), 0) == col).astype(jnp.bfloat16)
    acc_ref[...] += lax.dot_general(
        left, right, (((1,), (1,)), ((), ())), preferred_element_type=jnp.float32
    )


def local_kernel(count_ref, p_ref, c_ref, o_ref):
    step = pl.program_id(0)
    first = local_start(count_ref)

    @pl.when(step == 0)
    def _():
        o_ref[...] = jnp.zeros(o_ref.shape, o_ref.dtype)

    @pl.when(step * BLOCK + BLOCK > first)
    def _():
        accumulate(first, BLOCK, step, p_ref[...], c_ref[...], o_ref)


def arrived_kernel(block, x_ref, y_ref, a_ref, o_ref):
    o_ref[...] = a_ref[...]
    for source in (x_ref, y_ref):
        x = source[...]
        accumulate(0, block, 0, x[0:4], x[4:7].astype(jnp.int32), o_ref)


ACC_SHAPE = (4 * SPLITS * ROWS, COLS)


def deposit_local(payload, cells, counts):
    pick = lambda b, f: (0, jnp.maximum(b, local_start(f) // BLOCK))
    return pl.pallas_call(
        local_kernel,
        grid_spec=pltpu.PrefetchScalarGridSpec(
            num_scalar_prefetch=1,
            grid=(payload.shape[1] // BLOCK,),
            in_specs=[pl.BlockSpec((4, BLOCK), pick), pl.BlockSpec((3, BLOCK), pick)],
            out_specs=pl.BlockSpec(ACC_SHAPE, lambda b, f: (0, 0)),
        ),
        out_shape=jax.ShapeDtypeStruct(ACC_SHAPE, jnp.float32),
        compiler_params=pltpu.CompilerParams(dimension_semantics=("arbitrary",)),
    )(counts, payload, cells)


def deposit_arrived(first, second, acc, block):
    return pl.pallas_call(
        lambda x, y, a, o: arrived_kernel(block, x, y, a, o),
        grid=(1,),
        in_specs=[
            pl.BlockSpec((7, block), lambda b: (0, 0)),
            pl.BlockSpec((7, block), lambda b: (0, 0)),
            pl.BlockSpec(ACC_SHAPE, lambda b: (0, 0)),
        ],
        out_specs=pl.BlockSpec(ACC_SHAPE, lambda b: (0, 0)),
        out_shape=jax.ShapeDtypeStruct(ACC_SHAPE, jnp.float32),
        input_output_aliases={2: 0},
    )(first, second, acc)


def pack_kernel(count_ref, p_ref, c_ref, plus_x, minus_x, plus_y, minus_y):
    face = CAP_F + LANE
    corner = CAP_D + LANE
    places = (
        (plus_x, 0), (minus_x, 0), (plus_y, 0), (minus_y, 0),
        (plus_x, face), (plus_x, face + corner), (minus_x, face), (minus_x, face + corner),
    )
    start = 0
    for which, (out_ref, column) in enumerate(places):
        tally = count_ref[0, which]
        width = face if which < 4 else corner
        base = pl.multiple_of((start // LANE) * LANE, LANE)
        offset = start - base
        p = p_ref[:, pl.ds(base, width)]
        c = c_ref[:, pl.ds(base, width)]
        lane = lax.broadcasted_iota(jnp.int32, (1, width), 1)
        living = (lane >= offset) & (lane < offset + tally)
        out_ref[0:1, column : column + width] = jnp.where(living, p[0:1], 0.0)
        out_ref[1:4, column : column + width] = p[1:4]
        out_ref[4:7, column : column + width] = c.astype(jnp.float32)
        start = start + tally


def pack(payload, cells, counts):
    face = CAP_F + LANE
    corner = CAP_D + LANE
    widths = (face + 2 * corner, face + 2 * corner, face, face)
    return pl.pallas_call(
        pack_kernel,
        in_specs=[
            pl.BlockSpec(memory_space=pltpu.SMEM),
            pl.BlockSpec(memory_space=pltpu.VMEM),
            pl.BlockSpec(memory_space=pltpu.VMEM),
        ],
        out_shape=[jax.ShapeDtypeStruct((7, w), jnp.float32) for w in widths],
    )(counts, payload, cells)


def towards(block, sx, sy):
    gx = lax.axis_size("gx")
    gy = lax.axis_size("gy")
    route = []
    for ix in range(gx):
        for iy in range(gy):
            route.append((ix * gy + iy, ((ix + sx) % gx) * gy + (iy + sy) % gy))
    return lax.ppermute(block, ("gx", "gy"), route)


def bordered_density(density):
    upper_x = towards(density[:, :HALO, :], -1, 0)
    lower_x = towards(density[:, CX - HALO :, :], 1, 0)
    wide = jnp.concatenate([density, upper_x, lower_x], axis=1)
    upper_y = towards(wide[:, :, :HALO], 0, -1)
    lower_y = towards(wide[:, :, CY - HALO :], 0, 1)
    gap = jnp.zeros((NZ, WIDE_X, WIDE_Y - CY - 2 * HALO), jnp.float32)
    return jnp.concatenate([wide, upper_y, gap, lower_y], axis=2)


def near(v):
    flat = jnp.zeros((1,) + v.shape[1:], v.dtype)
    up = jnp.concatenate([v[1:], flat], axis=0)
    down = jnp.concatenate([flat, v[:-1]], axis=0)
    return (
        up
        + down
        + pltpu.roll(v, WIDE_X - 1, 1)
        + pltpu.roll(v, 1, 1)
        + pltpu.roll(v, WIDE_Y - 1, 2)
        + pltpu.roll(v, 1, 2)
    )


def relax_kernel(d_ref, o_ref):
    density = d_ref[...]
    source = COUPLING * ((density + SMOOTHING * (near(density) - 6.0 * density)) - BACKGROUND)
    shape = density.shape
    parity = (
        lax.broadcasted_iota(jnp.int32, shape, 0)
        + lax.broadcasted_iota(jnp.int32, shape, 1)
        + lax.broadcasted_iota(jnp.int32, shape, 2)
    ) % 2
    field = jnp.zeros(shape, jnp.float32)
    for _ in range(SWEEPS):
        for colour in (0, 1):
            middle = field
            residual = (
                near(middle)
                - 6.0 * middle
                - SCREENING * middle
                - CUBIC_TERM * middle * middle * middle
                - source
            )
            slope = -6.0 - SCREENING - 3.0 * CUBIC_TERM * middle * middle
            field = jnp.where(parity == colour, middle - residual / slope, middle)
    o_ref[...] = field[:, :CX, :CY]


def relax(bordered):
    return pl.pallas_call(
        relax_kernel,
        out_shape=jax.ShapeDtypeStruct((NZ, CX, CY), jnp.float32),
    )(bordered)


def staged(payload, cells, counts):
    face = CAP_F + LANE
    corner = CAP_D + LANE
    plus_x, minus_x, plus_y, minus_y = pack(payload, cells, counts)
    from_minus_x = towards(plus_x, 1, 0)
    from_plus_x = towards(minus_x, -1, 0)
    total = deposit_local(payload, cells, counts)
    plus_y = jnp.concatenate(
        [plus_y, from_minus_x[:, face : face + corner], from_plus_x[:, face : face + corner]], axis=1
    )
    minus_y = jnp.concatenate(
        [minus_y, from_minus_x[:, face + corner :], from_plus_x[:, face + corner :]], axis=1
    )
    from_minus_y = towards(plus_y, 0, 1)
    from_plus_y = towards(minus_y, 0, -1)
    total = deposit_arrived(from_minus_x, from_plus_x, total, face)
    total = deposit_arrived(from_minus_y, from_plus_y, total, face + 2 * corner)
    total = total.reshape(SPLITS, 4, ROWS * COLS)
    interior = (total[0] + total[1]).reshape(4, NZ, CX, CY)
    density = interior[0]
    momentum = interior[1:]
    scalar_field = relax(bordered_density(density))
    return (scalar_field, momentum)


def solution(mesh):
    placed = (P(None, ("gx", "gy")), P(None, ("gx", "gy")), P(("gx", "gy"), None))
    return jax.shard_map(
        staged,
        mesh=mesh,
        in_specs=placed,
        out_specs=(P(None, "gx", "gy"), P(None, None, "gx", "gy")),
        check_vma=False,
    )
```

```python
import jax
import jax.numpy as jnp
from jax import lax
from jax.experimental import pallas as pl
from jax.experimental.pallas import tpu as pltpu
from jax.sharding import PartitionSpec as P

CX = 16
CY = 128
NZ = 8
SWEEPS = 4
CAP_F = 2048
CAP_D = 512


SCREENING = 0.5
CUBIC_TERM = 0.3
COUPLING = 1.5
SMOOTHING = 0.1
BACKGROUND = 1.0

HALO = 2 * SWEEPS
ROWS = 64
COLS = 256
SPLITS = 2
BLOCK = 2048
LANE = 128
WIDE_X = 2 * CX
WIDE_Y = 2 * CY


def local_start(count_ref):
    total = count_ref[0, 0]
    for edge in range(1, 8):
        total = total + count_ref[0, edge]
    return total


def accumulate(first, block, step, p, c, acc_ref):
    width = p.shape[1]
    masses = p[0:1]
    vals = jnp.concatenate([masses, masses * p[1:4]], axis=0)
    cell = (c[0:1] * CX + c[1:2]) * CY + c[2:3]
    position = step * block + lax.broadcasted_iota(jnp.int32, (1, width), 1)
    cell = jnp.where(position >= first, cell, -1)
    row = lax.shift_right_arithmetic(cell, 8)
    col = lax.bitwise_and(cell, COLS - 1)
    hi = vals.astype(jnp.bfloat16)
    lo = (vals - hi.astype(jnp.float32)).astype(jnp.bfloat16)
    parts = [q.astype(jnp.float32)[e : e + 1] for q in (hi, lo) for e in range(4)]
    row_hot = (lax.broadcasted_iota(jnp.int32, (ROWS, width), 0) == row).astype(jnp.float32)
    left = jnp.concatenate([(row_hot * part).astype(jnp.bfloat16) for part in parts], axis=0)
    right = (lax.broadcasted_iota(jnp.int32, (COLS, width), 0) == col).astype(jnp.bfloat16)
    acc_ref[...] += lax.dot_general(
        left, right, (((1,), (1,)), ((), ())), preferred_element_type=jnp.float32
    )


def local_kernel(count_ref, p_ref, c_ref, o_ref):
    step = pl.program_id(0)
    first = local_start(count_ref)

    @pl.when(step == 0)
    def _():
        o_ref[...] = jnp.zeros(o_ref.shape, o_ref.dtype)

    @pl.when(step * BLOCK + BLOCK > first)
    def _():
        accumulate(first, BLOCK, step, p_ref[...], c_ref[...], o_ref)


def arrived_kernel(block, x_ref, y_ref, a_ref, o_ref):
    o_ref[...] = a_ref[...]
    for source in (x_ref, y_ref):
        x = source[...]
        accumulate(0, block, 0, x[0:4], x[4:7].astype(jnp.int32), o_ref)


ACC_SHAPE = (4 * SPLITS * ROWS, COLS)


def deposit_local(payload, cells, counts):
    pick = lambda b, f: (0, jnp.maximum(b, local_start(f) // BLOCK))
    return pl.pallas_call(
        local_kernel,
        grid_spec=pltpu.PrefetchScalarGridSpec(
            num_scalar_prefetch=1,
            grid=(payload.shape[1] // BLOCK,),
            in_specs=[pl.BlockSpec((4, BLOCK), pick), pl.BlockSpec((3, BLOCK), pick)],
            out_specs=pl.BlockSpec(ACC_SHAPE, lambda b, f: (0, 0)),
        ),
        out_shape=jax.ShapeDtypeStruct(ACC_SHAPE, jnp.float32),
        compiler_params=pltpu.CompilerParams(dimension_semantics=("arbitrary",)),
    )(counts, payload, cells)


def deposit_arrived(first, second, acc, block):
    return pl.pallas_call(
        lambda x, y, a, o: arrived_kernel(block, x, y, a, o),
        grid=(1,),
        in_specs=[
            pl.BlockSpec((7, block), lambda b: (0, 0)),
            pl.BlockSpec((7, block), lambda b: (0, 0)),
            pl.BlockSpec(ACC_SHAPE, lambda b: (0, 0)),
        ],
        out_specs=pl.BlockSpec(ACC_SHAPE, lambda b: (0, 0)),
        out_shape=jax.ShapeDtypeStruct(ACC_SHAPE, jnp.float32),
        input_output_aliases={2: 0},
    )(first, second, acc)


def pack_kernel(count_ref, p_ref, c_ref, plus_x, minus_x, plus_y, minus_y):
    face = CAP_F + LANE
    corner = CAP_D + LANE
    places = (
        (plus_x, 0), (minus_x, 0), (plus_y, 0), (minus_y, 0),
        (plus_x, face), (plus_x, face + corner), (minus_x, face), (minus_x, face + corner),
    )
    start = 0
    for which, (out_ref, column) in enumerate(places):
        tally = count_ref[0, which]
        width = face if which < 4 else corner
        base = pl.multiple_of((start // LANE) * LANE, LANE)
        offset = start - base
        p = p_ref[:, pl.ds(base, width)]
        c = c_ref[:, pl.ds(base, width)]
        lane = lax.broadcasted_iota(jnp.int32, (1, width), 1)
        living = (lane >= offset) & (lane < offset + tally)
        out_ref[0:1, column : column + width] = jnp.where(living, p[0:1], 0.0)
        out_ref[1:4, column : column + width] = p[1:4]
        out_ref[4:7, column : column + width] = c.astype(jnp.float32)
        start = start + tally


def pack(payload, cells, counts):
    face = CAP_F + LANE
    corner = CAP_D + LANE
    widths = (face + 2 * corner, face + 2 * corner, face, face)
    return pl.pallas_call(
        pack_kernel,
        in_specs=[
            pl.BlockSpec(memory_space=pltpu.SMEM),
            pl.BlockSpec(memory_space=pltpu.VMEM),
            pl.BlockSpec(memory_space=pltpu.VMEM),
        ],
        out_shape=[jax.ShapeDtypeStruct((7, w), jnp.float32) for w in widths],
    )(counts, payload, cells)


def towards(block, sx, sy):
    gx = lax.axis_size("gx")
    gy = lax.axis_size("gy")
    route = []
    for ix in range(gx):
        for iy in range(gy):
            route.append((ix * gy + iy, ((ix + sx) % gx) * gy + (iy + sy) % gy))
    return lax.ppermute(block, ("gx", "gy"), route)


def bordered_density(density):
    upper_x = towards(density[:, :HALO, :], -1, 0)
    lower_x = towards(density[:, CX - HALO :, :], 1, 0)
    wide = jnp.concatenate([density, upper_x, lower_x], axis=1)
    upper_y = towards(wide[:, :, :HALO], 0, -1)
    lower_y = towards(wide[:, :, CY - HALO :], 0, 1)
    return (density, upper_x, lower_x, upper_y, lower_y)


def near(v):
    flat = jnp.zeros((1,) + v.shape[1:], v.dtype)
    up = jnp.concatenate([v[1:], flat], axis=0)
    down = jnp.concatenate([flat, v[:-1]], axis=0)
    return (
        up
        + down
        + pltpu.roll(v, WIDE_X - 1, 1)
        + pltpu.roll(v, 1, 1)
        + pltpu.roll(v, WIDE_Y - 1, 2)
        + pltpu.roll(v, 1, 2)
    )


def relax_kernel(d_ref, ux_ref, lx_ref, uy_ref, ly_ref, o_ref, b_ref):
    b_ref[...] = jnp.zeros(b_ref.shape, jnp.float32)
    b_ref[:, 0:CX, 0:CY] = d_ref[...]
    b_ref[:, CX : CX + HALO, 0:CY] = ux_ref[...]
    b_ref[:, CX + HALO :, 0:CY] = lx_ref[...]
    b_ref[:, :, CY : CY + HALO] = uy_ref[...]
    b_ref[:, :, WIDE_Y - HALO :] = ly_ref[...]
    density = b_ref[...]
    source = COUPLING * ((density + SMOOTHING * (near(density) - 6.0 * density)) - BACKGROUND)
    shape = density.shape
    parity = (
        lax.broadcasted_iota(jnp.int32, shape, 0)
        + lax.broadcasted_iota(jnp.int32, shape, 1)
        + lax.broadcasted_iota(jnp.int32, shape, 2)
    ) % 2
    field = jnp.zeros(shape, jnp.float32)
    for _ in range(SWEEPS):
        for colour in (0, 1):
            middle = field
            residual = (
                near(middle)
                - 6.0 * middle
                - SCREENING * middle
                - CUBIC_TERM * middle * middle * middle
                - source
            )
            slope = -6.0 - SCREENING - 3.0 * CUBIC_TERM * middle * middle
            field = jnp.where(parity == colour, middle - residual / slope, middle)
    o_ref[...] = field[:, :CX, :CY]


def relax(pieces):
    return pl.pallas_call(
        relax_kernel,
        out_shape=jax.ShapeDtypeStruct((NZ, CX, CY), jnp.float32),
        scratch_shapes=[pltpu.VMEM((NZ, WIDE_X, WIDE_Y), jnp.float32)],
    )(*pieces)


def staged(payload, cells, counts):
    face = CAP_F + LANE
    corner = CAP_D + LANE
    plus_x, minus_x, plus_y, minus_y = pack(payload, cells, counts)
    from_minus_x = towards(plus_x, 1, 0)
    from_plus_x = towards(minus_x, -1, 0)
    total = deposit_local(payload, cells, counts)
    plus_y = jnp.concatenate(
        [plus_y, from_minus_x[:, face : face + corner], from_plus_x[:, face : face + corner]], axis=1
    )
    minus_y = jnp.concatenate(
        [minus_y, from_minus_x[:, face + corner :], from_plus_x[:, face + corner :]], axis=1
    )
    from_minus_y = towards(plus_y, 0, 1)
    from_plus_y = towards(minus_y, 0, -1)
    total = deposit_arrived(from_minus_x, from_plus_x, total, face)
    total = deposit_arrived(from_minus_y, from_plus_y, total, face + 2 * corner)
    total = total.reshape(SPLITS, 4, ROWS * COLS)
    density = (total[0, 0] + total[1, 0]).reshape(NZ, CX, CY)
    scalar_field = relax(bordered_density(density))
    momentum = (total[0, 1:] + total[1, 1:]).reshape(3, NZ, CX, CY)
    return (scalar_field, momentum)


def solution(mesh):
    placed = (P(None, ("gx", "gy")), P(None, ("gx", "gy")), P(("gx", "gy"), None))
    return jax.shard_map(
        staged,
        mesh=mesh,
        in_specs=placed,
        out_specs=(P(None, "gx", "gy"), P(None, None, "gx", "gy")),
        check_vma=False,
    )
```

```python
import jax
import jax.numpy as jnp
from jax import lax
from jax.experimental import pallas as pl
from jax.experimental.pallas import tpu as pltpu
from jax.sharding import PartitionSpec as P

CX = 16
CY = 128
NZ = 8
SWEEPS = 4
CAP_F = 2048
CAP_D = 512


SCREENING = 0.5
CUBIC_TERM = 0.3
COUPLING = 1.5
SMOOTHING = 0.1
BACKGROUND = 1.0

HALO = 2 * SWEEPS
ROWS = 64
COLS = 256
SPLITS = 2
BLOCK = 2048
LANE = 128
WIDE_X = 2 * CX
WIDE_Y = 2 * CY


def local_start(count_ref):
    total = count_ref[0, 0]
    for edge in range(1, 8):
        total = total + count_ref[0, edge]
    return total


def accumulate(first, block, step, p, c, acc_ref):
    width = p.shape[1]
    masses = p[0:1]
    vals = jnp.concatenate([masses, masses * p[1:4]], axis=0)
    position = step * block + lax.broadcasted_iota(jnp.int32, (1, width), 1)
    row = lax.shift_right_logical(c[0:1], 1) * CX + c[1:2]
    row = jnp.where(position >= first, row, -1)
    col = lax.bitwise_and(c[0:1], 1) * CY + c[2:3]
    hi = vals.astype(jnp.bfloat16)
    lo = (vals - hi.astype(jnp.float32)).astype(jnp.bfloat16)
    parts = [q.astype(jnp.float32)[e : e + 1] for q in (hi, lo) for e in range(4)]
    row_hot = (lax.broadcasted_iota(jnp.int32, (ROWS, width), 0) == row).astype(jnp.float32)
    left = jnp.concatenate([(row_hot * part).astype(jnp.bfloat16) for part in parts], axis=0)
    right = (lax.broadcasted_iota(jnp.int32, (COLS, width), 0) == col).astype(jnp.bfloat16)
    acc_ref[...] += lax.dot_general(
        left, right, (((1,), (1,)), ((), ())), preferred_element_type=jnp.float32
    )


def local_kernel(count_ref, p_ref, c_ref, o_ref):
    step = pl.program_id(0)
    first = local_start(count_ref)

    @pl.when(step == 0)
    def _():
        o_ref[...] = jnp.zeros(o_ref.shape, o_ref.dtype)

    @pl.when(step * BLOCK + BLOCK > first)
    def _():
        accumulate(first, BLOCK, step, p_ref[...], c_ref[...], o_ref)


def arrived_kernel(block, x_ref, y_ref, a_ref, o_ref):
    o_ref[...] = a_ref[...]
    for source in (x_ref, y_ref):
        x = source[...]
        accumulate(0, block, 0, x[0:4], x[4:7].astype(jnp.int32), o_ref)


ACC_SHAPE = (4 * SPLITS * ROWS, COLS)


def deposit_local(payload, cells, counts):
    pick = lambda b, f: (0, jnp.maximum(b, local_start(f) // BLOCK))
    return pl.pallas_call(
        local_kernel,
        grid_spec=pltpu.PrefetchScalarGridSpec(
            num_scalar_prefetch=1,
            grid=(payload.shape[1] // BLOCK,),
            in_specs=[pl.BlockSpec((4, BLOCK), pick), pl.BlockSpec((3, BLOCK), pick)],
            out_specs=pl.BlockSpec(ACC_SHAPE, lambda b, f: (0, 0)),
        ),
        out_shape=jax.ShapeDtypeStruct(ACC_SHAPE, jnp.float32),
        compiler_params=pltpu.CompilerParams(dimension_semantics=("arbitrary",)),
    )(counts, payload, cells)


def deposit_arrived(first, second, acc, block):
    return pl.pallas_call(
        lambda x, y, a, o: arrived_kernel(block, x, y, a, o),
        grid=(1,),
        in_specs=[
            pl.BlockSpec((7, block), lambda b: (0, 0)),
            pl.BlockSpec((7, block), lambda b: (0, 0)),
            pl.BlockSpec(ACC_SHAPE, lambda b: (0, 0)),
        ],
        out_specs=pl.BlockSpec(ACC_SHAPE, lambda b: (0, 0)),
        out_shape=jax.ShapeDtypeStruct(ACC_SHAPE, jnp.float32),
        input_output_aliases={2: 0},
    )(first, second, acc)


def pack_kernel(count_ref, p_ref, c_ref, plus_x, minus_x, plus_y, minus_y):
    face = CAP_F + LANE
    corner = CAP_D + LANE
    places = (
        (plus_x, 0), (minus_x, 0), (plus_y, 0), (minus_y, 0),
        (plus_x, face), (plus_x, face + corner), (minus_x, face), (minus_x, face + corner),
    )
    start = 0
    for which, (out_ref, column) in enumerate(places):
        tally = count_ref[0, which]
        width = face if which < 4 else corner
        base = pl.multiple_of((start // LANE) * LANE, LANE)
        offset = start - base
        p = p_ref[:, pl.ds(base, width)]
        c = c_ref[:, pl.ds(base, width)]
        lane = lax.broadcasted_iota(jnp.int32, (1, width), 1)
        living = (lane >= offset) & (lane < offset + tally)
        out_ref[0:1, column : column + width] = jnp.where(living, p[0:1], 0.0)
        out_ref[1:4, column : column + width] = p[1:4]
        out_ref[4:7, column : column + width] = c.astype(jnp.float32)
        start = start + tally


def pack(payload, cells, counts):
    face = CAP_F + LANE
    corner = CAP_D + LANE
    widths = (face + 2 * corner, face + 2 * corner, face, face)
    return pl.pallas_call(
        pack_kernel,
        in_specs=[
            pl.BlockSpec(memory_space=pltpu.SMEM),
            pl.BlockSpec(memory_space=pltpu.VMEM),
            pl.BlockSpec(memory_space=pltpu.VMEM),
        ],
        out_shape=[jax.ShapeDtypeStruct((7, w), jnp.float32) for w in widths],
    )(counts, payload, cells)


def towards(block, sx, sy):
    gx = lax.axis_size("gx")
    gy = lax.axis_size("gy")
    route = []
    for ix in range(gx):
        for iy in range(gy):
            route.append((ix * gy + iy, ((ix + sx) % gx) * gy + (iy + sy) % gy))
    return lax.ppermute(block, ("gx", "gy"), route)


def bordered_density(density):
    upper_x = towards(density[:, :HALO, :], -1, 0)
    lower_x = towards(density[:, CX - HALO :, :], 1, 0)
    wide = jnp.concatenate([density, upper_x, lower_x], axis=1)
    upper_y = towards(wide[:, :, :HALO], 0, -1)
    lower_y = towards(wide[:, :, CY - HALO :], 0, 1)
    return (density, upper_x, lower_x, upper_y, lower_y)


def near(v):
    flat = jnp.zeros((1,) + v.shape[1:], v.dtype)
    up = jnp.concatenate([v[1:], flat], axis=0)
    down = jnp.concatenate([flat, v[:-1]], axis=0)
    return (
        up
        + down
        + pltpu.roll(v, WIDE_X - 1, 1)
        + pltpu.roll(v, 1, 1)
        + pltpu.roll(v, WIDE_Y - 1, 2)
        + pltpu.roll(v, 1, 2)
    )


def relax_kernel(d_ref, ux_ref, lx_ref, uy_ref, ly_ref, o_ref, b_ref):
    b_ref[...] = jnp.zeros(b_ref.shape, jnp.float32)
    b_ref[:, 0:CX, 0:CY] = d_ref[...]
    b_ref[:, CX : CX + HALO, 0:CY] = ux_ref[...]
    b_ref[:, CX + HALO :, 0:CY] = lx_ref[...]
    b_ref[:, :, CY : CY + HALO] = uy_ref[...]
    b_ref[:, :, WIDE_Y - HALO :] = ly_ref[...]
    density = b_ref[...]
    source = COUPLING * ((density + SMOOTHING * (near(density) - 6.0 * density)) - BACKGROUND)
    shape = density.shape
    parity = (
        lax.broadcasted_iota(jnp.int32, shape, 0)
        + lax.broadcasted_iota(jnp.int32, shape, 1)
        + lax.broadcasted_iota(jnp.int32, shape, 2)
    ) % 2
    field = jnp.zeros(shape, jnp.float32)
    for _ in range(SWEEPS):
        for colour in (0, 1):
            middle = field
            residual = (
                near(middle)
                - 6.0 * middle
                - SCREENING * middle
                - CUBIC_TERM * middle * middle * middle
                - source
            )
            slope = -6.0 - SCREENING - 3.0 * CUBIC_TERM * middle * middle
            field = jnp.where(parity == colour, middle - residual / slope, middle)
    o_ref[...] = field[:, :CX, :CY]


def relax(pieces):
    return pl.pallas_call(
        relax_kernel,
        out_shape=jax.ShapeDtypeStruct((NZ, CX, CY), jnp.float32),
        scratch_shapes=[pltpu.VMEM((NZ, WIDE_X, WIDE_Y), jnp.float32)],
    )(*pieces)


def staged(payload, cells, counts):
    face = CAP_F + LANE
    corner = CAP_D + LANE
    plus_x, minus_x, plus_y, minus_y = pack(payload, cells, counts)
    from_minus_x = towards(plus_x, 1, 0)
    from_plus_x = towards(minus_x, -1, 0)
    total = deposit_local(payload, cells, counts)
    plus_y = jnp.concatenate(
        [plus_y, from_minus_x[:, face : face + corner], from_plus_x[:, face : face + corner]], axis=1
    )
    minus_y = jnp.concatenate(
        [minus_y, from_minus_x[:, face + corner :], from_plus_x[:, face + corner :]], axis=1
    )
    from_minus_y = towards(plus_y, 0, 1)
    from_plus_y = towards(minus_y, 0, -1)
    total = deposit_arrived(from_minus_x, from_plus_x, total, face)
    total = deposit_arrived(from_minus_y, from_plus_y, total, face + 2 * corner)
    total = total.reshape(SPLITS, 4, NZ // 2, CX, 2 * CY)
    summed = total[0, 0] + total[1, 0]
    density = jnp.stack([summed[..., :CY], summed[..., CY:]], axis=1).reshape(NZ, CX, CY)
    scalar_field = relax(bordered_density(density))
    summed = total[0, 1:] + total[1, 1:]
    momentum = jnp.stack([summed[..., :CY], summed[..., CY:]], axis=2).reshape(3, NZ, CX, CY)
    return (scalar_field, momentum)


def solution(mesh):
    placed = (P(None, ("gx", "gy")), P(None, ("gx", "gy")), P(("gx", "gy"), None))
    return jax.shard_map(
        staged,
        mesh=mesh,
        in_specs=placed,
        out_specs=(P(None, "gx", "gy"), P(None, None, "gx", "gy")),
        check_vma=False,
    )
```

```python
import jax
import jax.numpy as jnp
from jax import lax
from jax.experimental import pallas as pl
from jax.experimental.pallas import tpu as pltpu
from jax.sharding import PartitionSpec as P

CX = 16
CY = 128
NZ = 8
SWEEPS = 4
CAP_F = 2048
CAP_D = 512


SCREENING = 0.5
CUBIC_TERM = 0.3
COUPLING = 1.5
SMOOTHING = 0.1
BACKGROUND = 1.0

HALO = 2 * SWEEPS
ROWS = 64
COLS = 256
SPLITS = 2
BLOCK = 2048
LANE = 128
WIDE_X = 2 * CX
WIDE_Y = 2 * CY


def local_start(count_ref):
    total = count_ref[0, 0]
    for edge in range(1, 8):
        total = total + count_ref[0, edge]
    return total


def accumulate(first, block, step, p, c, acc_ref):
    width = p.shape[1]
    masses = p[0:1]
    vals = jnp.concatenate([masses, masses * p[1:4]], axis=0)
    position = step * block + lax.broadcasted_iota(jnp.int32, (1, width), 1)
    row = lax.shift_right_logical(c[0:1], 1) * CX + c[1:2]
    row = jnp.where(position >= first, row, -1)
    col = lax.bitwise_and(c[0:1], 1) * CY + c[2:3]
    hi = vals.astype(jnp.bfloat16)
    lo = (vals - hi.astype(jnp.float32)).astype(jnp.bfloat16)
    parts = [q.astype(jnp.float32)[e : e + 1] for q in (hi, lo) for e in range(4)]
    row_hot = (lax.broadcasted_iota(jnp.int32, (ROWS, width), 0) == row).astype(jnp.float32)
    left = jnp.concatenate([(row_hot * part).astype(jnp.bfloat16) for part in parts], axis=0)
    right = (lax.broadcasted_iota(jnp.int32, (COLS, width), 0) == col).astype(jnp.bfloat16)
    acc_ref[...] += lax.dot_general(
        left, right, (((1,), (1,)), ((), ())), preferred_element_type=jnp.float32
    )


def local_kernel(count_ref, p_ref, c_ref, o_ref):
    step = pl.program_id(0)
    first = local_start(count_ref)

    @pl.when(step == 0)
    def _():
        o_ref[...] = jnp.zeros(o_ref.shape, o_ref.dtype)

    @pl.when(step * BLOCK + BLOCK > first)
    def _():
        accumulate(first, BLOCK, step, p_ref[...], c_ref[...], o_ref)


def arrived_kernel(block, *refs):
    a_ref, o_ref = refs[-2], refs[-1]
    o_ref[...] = a_ref[...]
    for source in refs[:-2]:
        x = source[...]
        accumulate(0, block, 0, x[0:4], x[4:7].astype(jnp.int32), o_ref)


ACC_SHAPE = (4 * SPLITS * ROWS, COLS)


def deposit_local(payload, cells, counts):
    pick = lambda b, f: (0, jnp.maximum(b, local_start(f) // BLOCK))
    return pl.pallas_call(
        local_kernel,
        grid_spec=pltpu.PrefetchScalarGridSpec(
            num_scalar_prefetch=1,
            grid=(payload.shape[1] // BLOCK,),
            in_specs=[pl.BlockSpec((4, BLOCK), pick), pl.BlockSpec((3, BLOCK), pick)],
            out_specs=pl.BlockSpec(ACC_SHAPE, lambda b, f: (0, 0)),
        ),
        out_shape=jax.ShapeDtypeStruct(ACC_SHAPE, jnp.float32),
        compiler_params=pltpu.CompilerParams(dimension_semantics=("arbitrary",)),
    )(counts, payload, cells)


def deposit_arrived(sources, acc, block):
    count = len(sources)
    return pl.pallas_call(
        lambda *refs: arrived_kernel(block, *refs),
        grid=(1,),
        in_specs=[pl.BlockSpec((7, block), lambda b: (0, 0)) for source in sources]
        + [pl.BlockSpec(ACC_SHAPE, lambda b: (0, 0))],
        out_specs=pl.BlockSpec(ACC_SHAPE, lambda b: (0, 0)),
        out_shape=jax.ShapeDtypeStruct(ACC_SHAPE, jnp.float32),
        input_output_aliases={count: 0},
    )(*sources, acc)


def pack_kernel(count_ref, p_ref, c_ref, plus_x, minus_x, plus_y, minus_y):
    face = CAP_F + LANE
    corner = CAP_D + LANE
    places = (
        (plus_x, 0), (minus_x, 0), (plus_y, 0), (minus_y, 0),
        (plus_x, face), (plus_x, face + corner), (minus_x, face), (minus_x, face + corner),
    )
    start = 0
    for which, (out_ref, column) in enumerate(places):
        tally = count_ref[0, which]
        width = face if which < 4 else corner
        base = pl.multiple_of((start // LANE) * LANE, LANE)
        offset = start - base
        p = p_ref[:, pl.ds(base, width)]
        c = c_ref[:, pl.ds(base, width)]
        lane = lax.broadcasted_iota(jnp.int32, (1, width), 1)
        living = (lane >= offset) & (lane < offset + tally)
        out_ref[0:1, column : column + width] = jnp.where(living, p[0:1], 0.0)
        out_ref[1:4, column : column + width] = p[1:4]
        out_ref[4:7, column : column + width] = c.astype(jnp.float32)
        start = start + tally


def pack(payload, cells, counts):
    face = CAP_F + LANE
    corner = CAP_D + LANE
    widths = (face + 2 * corner, face + 2 * corner, face, face)
    return pl.pallas_call(
        pack_kernel,
        in_specs=[
            pl.BlockSpec(memory_space=pltpu.SMEM),
            pl.BlockSpec(memory_space=pltpu.VMEM),
            pl.BlockSpec(memory_space=pltpu.VMEM),
        ],
        out_shape=[jax.ShapeDtypeStruct((7, w), jnp.float32) for w in widths],
    )(counts, payload, cells)


def towards(block, sx, sy):
    gx = lax.axis_size("gx")
    gy = lax.axis_size("gy")
    route = []
    for ix in range(gx):
        for iy in range(gy):
            route.append((ix * gy + iy, ((ix + sx) % gx) * gy + (iy + sy) % gy))
    return lax.ppermute(block, ("gx", "gy"), route)


def bordered_density(density):
    upper_x = towards(density[:, :HALO, :], -1, 0)
    lower_x = towards(density[:, CX - HALO :, :], 1, 0)
    wide = jnp.concatenate([density, upper_x, lower_x], axis=1)
    upper_y = towards(wide[:, :, :HALO], 0, -1)
    lower_y = towards(wide[:, :, CY - HALO :], 0, 1)
    return (density, upper_x, lower_x, upper_y, lower_y)


def near(v):
    flat = jnp.zeros((1,) + v.shape[1:], v.dtype)
    up = jnp.concatenate([v[1:], flat], axis=0)
    down = jnp.concatenate([flat, v[:-1]], axis=0)
    return (
        up
        + down
        + pltpu.roll(v, WIDE_X - 1, 1)
        + pltpu.roll(v, 1, 1)
        + pltpu.roll(v, WIDE_Y - 1, 2)
        + pltpu.roll(v, 1, 2)
    )


def relax_kernel(d_ref, ux_ref, lx_ref, uy_ref, ly_ref, o_ref, b_ref):
    b_ref[...] = jnp.zeros(b_ref.shape, jnp.float32)
    b_ref[:, 0:CX, 0:CY] = d_ref[...]
    b_ref[:, CX : CX + HALO, 0:CY] = ux_ref[...]
    b_ref[:, CX + HALO :, 0:CY] = lx_ref[...]
    b_ref[:, :, CY : CY + HALO] = uy_ref[...]
    b_ref[:, :, WIDE_Y - HALO :] = ly_ref[...]
    density = b_ref[...]
    source = COUPLING * ((density + SMOOTHING * (near(density) - 6.0 * density)) - BACKGROUND)
    shape = density.shape
    parity = (
        lax.broadcasted_iota(jnp.int32, shape, 0)
        + lax.broadcasted_iota(jnp.int32, shape, 1)
        + lax.broadcasted_iota(jnp.int32, shape, 2)
    ) % 2
    field = jnp.zeros(shape, jnp.float32)
    for _ in range(SWEEPS):
        for colour in (0, 1):
            middle = field
            residual = (
                near(middle)
                - 6.0 * middle
                - SCREENING * middle
                - CUBIC_TERM * middle * middle * middle
                - source
            )
            slope = -6.0 - SCREENING - 3.0 * CUBIC_TERM * middle * middle
            field = jnp.where(parity == colour, middle - residual / slope, middle)
    o_ref[...] = field[:, :CX, :CY]


def relax(pieces):
    return pl.pallas_call(
        relax_kernel,
        out_shape=jax.ShapeDtypeStruct((NZ, CX, CY), jnp.float32),
        scratch_shapes=[pltpu.VMEM((NZ, WIDE_X, WIDE_Y), jnp.float32)],
    )(*pieces)


def staged(payload, cells, counts):
    face = CAP_F + LANE
    corner = CAP_D + LANE
    plus_x, minus_x, plus_y, minus_y = pack(payload, cells, counts)
    from_minus_x = towards(plus_x, 1, 0)
    from_plus_x = towards(minus_x, -1, 0)
    from_minus_y = towards(plus_y, 0, 1)
    from_plus_y = towards(minus_y, 0, -1)
    total = deposit_local(payload, cells, counts)
    upward = jnp.concatenate(
        [from_minus_x[:, face : face + corner], from_plus_x[:, face : face + corner]], axis=1
    )
    downward = jnp.concatenate([from_minus_x[:, face + corner :], from_plus_x[:, face + corner :]], axis=1)
    corners_below = towards(upward, 0, 1)
    corners_above = towards(downward, 0, -1)
    total = deposit_arrived((from_minus_x, from_plus_x, from_minus_y, from_plus_y), total, face)
    total = deposit_arrived((corners_below, corners_above), total, 2 * corner)
    total = total.reshape(SPLITS, 4, NZ // 2, CX, 2 * CY)
    summed = total[0, 0] + total[1, 0]
    density = jnp.stack([summed[..., :CY], summed[..., CY:]], axis=1).reshape(NZ, CX, CY)
    scalar_field = relax(bordered_density(density))
    summed = total[0, 1:] + total[1, 1:]
    momentum = jnp.stack([summed[..., :CY], summed[..., CY:]], axis=2).reshape(3, NZ, CX, CY)
    return (scalar_field, momentum)


def solution(mesh):
    placed = (P(None, ("gx", "gy")), P(None, ("gx", "gy")), P(("gx", "gy"), None))
    return jax.shard_map(
        staged,
        mesh=mesh,
        in_specs=placed,
        out_specs=(P(None, "gx", "gy"), P(None, None, "gx", "gy")),
        check_vma=False,
    )
```

```python
import jax
import jax.numpy as jnp
from jax import lax
from jax.experimental import pallas as pl
from jax.experimental.pallas import tpu as pltpu
from jax.sharding import PartitionSpec as P

CX = 16
CY = 128
NZ = 8
SWEEPS = 4
CAP_F = 2048
CAP_D = 512
MY = 16


SCREENING = 0.5
CUBIC_TERM = 0.3
COUPLING = 1.5
SMOOTHING = 0.1
BACKGROUND = 1.0

HALO = 2 * SWEEPS
ROWS = 64
COLS = 256
SPLITS = 2
BLOCK = 2048
LANE = 128
WIDE_X = 2 * CX
WIDE_Y = 2 * CY


def local_start(count_ref):
    total = count_ref[0, 0]
    for edge in range(1, 8):
        total = total + count_ref[0, edge]
    return total


def accumulate(first, block, step, p, c, acc_ref):
    width = p.shape[1]
    masses = p[0:1]
    vals = jnp.concatenate([masses, masses * p[1:4]], axis=0)
    position = step * block + lax.broadcasted_iota(jnp.int32, (1, width), 1)
    row = lax.shift_right_logical(c[0:1], 1) * CX + c[1:2]
    row = jnp.where(position >= first, row, -1)
    col = lax.bitwise_and(c[0:1], 1) * CY + c[2:3]
    hi = vals.astype(jnp.bfloat16)
    lo = (vals - hi.astype(jnp.float32)).astype(jnp.bfloat16)
    parts = [q.astype(jnp.float32)[e : e + 1] for q in (hi, lo) for e in range(4)]
    row_hot = (lax.broadcasted_iota(jnp.int32, (ROWS, width), 0) == row).astype(jnp.float32)
    left = jnp.concatenate([(row_hot * part).astype(jnp.bfloat16) for part in parts], axis=0)
    right = (lax.broadcasted_iota(jnp.int32, (COLS, width), 0) == col).astype(jnp.bfloat16)
    acc_ref[...] += lax.dot_general(
        left, right, (((1,), (1,)), ((), ())), preferred_element_type=jnp.float32
    )


def crossing_kernel(x_ref, y_ref, a_ref, o_ref):
    o_ref[...] = a_ref[...]
    for source, low in ((x_ref, 0), (y_ref, CY - MY)):
        x = source[...]
        p = x[0:4]
        c = x[4:7].astype(jnp.int32)
        width = p.shape[1]
        masses = p[0:1]
        vals = jnp.concatenate([masses, masses * p[1:4]], axis=0)
        row = lax.shift_right_logical(c[0:1], 1) * CX + c[1:2]
        near_j = c[2:3] - low
        row = jnp.where((near_j >= 0) & (near_j < MY), row, -1)
        col = lax.bitwise_and(c[0:1], 1) * MY + near_j
        hi = vals.astype(jnp.bfloat16)
        lo = (vals - hi.astype(jnp.float32)).astype(jnp.bfloat16)
        parts = [q.astype(jnp.float32)[e : e + 1] for q in (hi, lo) for e in range(4)]
        row_hot = (lax.broadcasted_iota(jnp.int32, (ROWS, width), 0) == row).astype(jnp.float32)
        left = jnp.concatenate([(row_hot * part).astype(jnp.bfloat16) for part in parts], axis=0)
        right = (lax.broadcasted_iota(jnp.int32, (2 * MY, width), 0) == col).astype(jnp.bfloat16)
        part = lax.dot_general(
            left, right, (((1,), (1,)), ((), ())), preferred_element_type=jnp.float32
        )
        o_ref[:, low : low + MY] += part[:, 0:MY]
        o_ref[:, CY + low : CY + low + MY] += part[:, MY:]


def deposit_crossing(first, second, acc):
    block = first.shape[1]
    return pl.pallas_call(
        crossing_kernel,
        grid=(1,),
        in_specs=[
            pl.BlockSpec((7, block), lambda b: (0, 0)),
            pl.BlockSpec((7, block), lambda b: (0, 0)),
            pl.BlockSpec(ACC_SHAPE, lambda b: (0, 0)),
        ],
        out_specs=pl.BlockSpec(ACC_SHAPE, lambda b: (0, 0)),
        out_shape=jax.ShapeDtypeStruct(ACC_SHAPE, jnp.float32),
        input_output_aliases={2: 0},
    )(first, second, acc)


def local_kernel(count_ref, p_ref, c_ref, o_ref):
    step = pl.program_id(0)
    first = local_start(count_ref)

    @pl.when(step == 0)
    def _():
        o_ref[...] = jnp.zeros(o_ref.shape, o_ref.dtype)

    @pl.when(step * BLOCK + BLOCK > first)
    def _():
        accumulate(first, BLOCK, step, p_ref[...], c_ref[...], o_ref)


def arrived_kernel(block, x_ref, y_ref, a_ref, o_ref):
    o_ref[...] = a_ref[...]
    for source in (x_ref, y_ref):
        x = source[...]
        accumulate(0, block, 0, x[0:4], x[4:7].astype(jnp.int32), o_ref)


ACC_SHAPE = (4 * SPLITS * ROWS, COLS)


def deposit_local(payload, cells, counts):
    pick = lambda b, f: (0, jnp.maximum(b, local_start(f) // BLOCK))
    return pl.pallas_call(
        local_kernel,
        grid_spec=pltpu.PrefetchScalarGridSpec(
            num_scalar_prefetch=1,
            grid=(payload.shape[1] // BLOCK,),
            in_specs=[pl.BlockSpec((4, BLOCK), pick), pl.BlockSpec((3, BLOCK), pick)],
            out_specs=pl.BlockSpec(ACC_SHAPE, lambda b, f: (0, 0)),
        ),
        out_shape=jax.ShapeDtypeStruct(ACC_SHAPE, jnp.float32),
        compiler_params=pltpu.CompilerParams(dimension_semantics=("arbitrary",)),
    )(counts, payload, cells)


def deposit_arrived(first, second, acc, block):
    return pl.pallas_call(
        lambda x, y, a, o: arrived_kernel(block, x, y, a, o),
        grid=(1,),
        in_specs=[
            pl.BlockSpec((7, block), lambda b: (0, 0)),
            pl.BlockSpec((7, block), lambda b: (0, 0)),
            pl.BlockSpec(ACC_SHAPE, lambda b: (0, 0)),
        ],
        out_specs=pl.BlockSpec(ACC_SHAPE, lambda b: (0, 0)),
        out_shape=jax.ShapeDtypeStruct(ACC_SHAPE, jnp.float32),
        input_output_aliases={2: 0},
    )(first, second, acc)


def pack_kernel(count_ref, p_ref, c_ref, plus_x, minus_x, plus_y, minus_y):
    face = CAP_F + LANE
    corner = CAP_D + LANE
    places = (
        (plus_x, 0), (minus_x, 0), (plus_y, 0), (minus_y, 0),
        (plus_x, face), (plus_x, face + corner), (minus_x, face), (minus_x, face + corner),
    )
    start = 0
    for which, (out_ref, column) in enumerate(places):
        tally = count_ref[0, which]
        width = face if which < 4 else corner
        base = pl.multiple_of((start // LANE) * LANE, LANE)
        offset = start - base
        p = p_ref[:, pl.ds(base, width)]
        c = c_ref[:, pl.ds(base, width)]
        lane = lax.broadcasted_iota(jnp.int32, (1, width), 1)
        living = (lane >= offset) & (lane < offset + tally)
        out_ref[0:1, column : column + width] = jnp.where(living, p[0:1], 0.0)
        out_ref[1:4, column : column + width] = p[1:4]
        out_ref[4:7, column : column + width] = c.astype(jnp.float32)
        start = start + tally


def pack(payload, cells, counts):
    face = CAP_F + LANE
    corner = CAP_D + LANE
    widths = (face + 2 * corner, face + 2 * corner, face, face)
    return pl.pallas_call(
        pack_kernel,
        in_specs=[
            pl.BlockSpec(memory_space=pltpu.SMEM),
            pl.BlockSpec(memory_space=pltpu.VMEM),
            pl.BlockSpec(memory_space=pltpu.VMEM),
        ],
        out_shape=[jax.ShapeDtypeStruct((7, w), jnp.float32) for w in widths],
    )(counts, payload, cells)


def towards(block, sx, sy):
    gx = lax.axis_size("gx")
    gy = lax.axis_size("gy")
    route = []
    for ix in range(gx):
        for iy in range(gy):
            route.append((ix * gy + iy, ((ix + sx) % gx) * gy + (iy + sy) % gy))
    return lax.ppermute(block, ("gx", "gy"), route)


def bordered_density(density):
    upper_x = towards(density[:, :HALO, :], -1, 0)
    lower_x = towards(density[:, CX - HALO :, :], 1, 0)
    wide = jnp.concatenate([density, upper_x, lower_x], axis=1)
    upper_y = towards(wide[:, :, :HALO], 0, -1)
    lower_y = towards(wide[:, :, CY - HALO :], 0, 1)
    return (density, upper_x, lower_x, upper_y, lower_y)


def near(v):
    flat = jnp.zeros((1,) + v.shape[1:], v.dtype)
    up = jnp.concatenate([v[1:], flat], axis=0)
    down = jnp.concatenate([flat, v[:-1]], axis=0)
    return (
        up
        + down
        + pltpu.roll(v, WIDE_X - 1, 1)
        + pltpu.roll(v, 1, 1)
        + pltpu.roll(v, WIDE_Y - 1, 2)
        + pltpu.roll(v, 1, 2)
    )


def relax_kernel(d_ref, ux_ref, lx_ref, uy_ref, ly_ref, o_ref, b_ref):
    b_ref[...] = jnp.zeros(b_ref.shape, jnp.float32)
    b_ref[:, 0:CX, 0:CY] = d_ref[...]
    b_ref[:, CX : CX + HALO, 0:CY] = ux_ref[...]
    b_ref[:, CX + HALO :, 0:CY] = lx_ref[...]
    b_ref[:, :, CY : CY + HALO] = uy_ref[...]
    b_ref[:, :, WIDE_Y - HALO :] = ly_ref[...]
    density = b_ref[...]
    source = COUPLING * ((density + SMOOTHING * (near(density) - 6.0 * density)) - BACKGROUND)
    shape = density.shape
    parity = (
        lax.broadcasted_iota(jnp.int32, shape, 0)
        + lax.broadcasted_iota(jnp.int32, shape, 1)
        + lax.broadcasted_iota(jnp.int32, shape, 2)
    ) % 2
    field = jnp.zeros(shape, jnp.float32)
    for _ in range(SWEEPS):
        for colour in (0, 1):
            middle = field
            residual = (
                near(middle)
                - 6.0 * middle
                - SCREENING * middle
                - CUBIC_TERM * middle * middle * middle
                - source
            )
            slope = -6.0 - SCREENING - 3.0 * CUBIC_TERM * middle * middle
            field = jnp.where(parity == colour, middle - residual / slope, middle)
    o_ref[...] = field[:, :CX, :CY]


def relax(pieces):
    return pl.pallas_call(
        relax_kernel,
        out_shape=jax.ShapeDtypeStruct((NZ, CX, CY), jnp.float32),
        scratch_shapes=[pltpu.VMEM((NZ, WIDE_X, WIDE_Y), jnp.float32)],
    )(*pieces)


def staged(payload, cells, counts):
    face = CAP_F + LANE
    corner = CAP_D + LANE
    plus_x, minus_x, plus_y, minus_y = pack(payload, cells, counts)
    from_minus_x = towards(plus_x, 1, 0)
    from_plus_x = towards(minus_x, -1, 0)
    total = deposit_local(payload, cells, counts)
    plus_y = jnp.concatenate(
        [plus_y, from_minus_x[:, face : face + corner], from_plus_x[:, face : face + corner]], axis=1
    )
    minus_y = jnp.concatenate(
        [minus_y, from_minus_x[:, face + corner :], from_plus_x[:, face + corner :]], axis=1
    )
    from_minus_y = towards(plus_y, 0, 1)
    from_plus_y = towards(minus_y, 0, -1)
    total = deposit_arrived(from_minus_x, from_plus_x, total, face)
    total = deposit_crossing(from_minus_y, from_plus_y, total)
    total = total.reshape(SPLITS, 4, NZ // 2, CX, 2 * CY)
    summed = total[0, 0] + total[1, 0]
    density = jnp.stack([summed[..., :CY], summed[..., CY:]], axis=1).reshape(NZ, CX, CY)
    scalar_field = relax(bordered_density(density))
    summed = total[0, 1:] + total[1, 1:]
    momentum = jnp.stack([summed[..., :CY], summed[..., CY:]], axis=2).reshape(3, NZ, CX, CY)
    return (scalar_field, momentum)


def solution(mesh):
    placed = (P(None, ("gx", "gy")), P(None, ("gx", "gy")), P(("gx", "gy"), None))
    return jax.shard_map(
        staged,
        mesh=mesh,
        in_specs=placed,
        out_specs=(P(None, "gx", "gy"), P(None, None, "gx", "gy")),
        check_vma=False,
    )
```

```python
import jax
import jax.numpy as jnp
from jax import lax
from jax.experimental import pallas as pl
from jax.experimental.pallas import tpu as pltpu
from jax.sharding import PartitionSpec as P

CX = 16
CY = 128
NZ = 8
SWEEPS = 4
CAP_F = 2048
CAP_D = 512


SCREENING = 0.5
CUBIC_TERM = 0.3
COUPLING = 1.5
SMOOTHING = 0.1
BACKGROUND = 1.0

HALO = 2 * SWEEPS
ROWS = 64
COLS = 256
SPLITS = 2
BLOCK = 2048
LANE = 128
WIDE_X = 2 * CX
WIDE_Y = 2 * CY


def local_start(count_ref):
    total = count_ref[0, 0]
    for edge in range(1, 8):
        total = total + count_ref[0, edge]
    return total


def accumulate(first, block, step, p, c, acc_ref):
    width = p.shape[1]
    masses = p[0:1]
    vals = jnp.concatenate([masses, masses * p[1:4]], axis=0)
    position = step * block + lax.broadcasted_iota(jnp.int32, (1, width), 1)
    row = lax.shift_right_logical(c[0:1], 1) * CX + c[1:2]
    row = jnp.where(position >= first, row, -1)
    col = lax.bitwise_and(c[0:1], 1) * CY + c[2:3]
    hi = vals.astype(jnp.bfloat16)
    lo = (vals - hi.astype(jnp.float32)).astype(jnp.bfloat16)
    parts = [q.astype(jnp.float32)[e : e + 1] for q in (hi, lo) for e in range(4)]
    row_hot = (lax.broadcasted_iota(jnp.int32, (ROWS, width), 0) == row).astype(jnp.float32)
    left = jnp.concatenate([(row_hot * part).astype(jnp.bfloat16) for part in parts], axis=0)
    right = (lax.broadcasted_iota(jnp.int32, (COLS, width), 0) == col).astype(jnp.bfloat16)
    acc_ref[...] += lax.dot_general(
        left, right, (((1,), (1,)), ((), ())), preferred_element_type=jnp.float32
    )


def local_kernel(count_ref, p_ref, c_ref, o_ref):
    step = pl.program_id(0)
    first = local_start(count_ref)

    @pl.when(step == 0)
    def _():
        o_ref[...] = jnp.zeros(o_ref.shape, o_ref.dtype)

    @pl.when(step * BLOCK + BLOCK > first)
    def _():
        accumulate(first, BLOCK, step, p_ref[...], c_ref[...], o_ref)


def arrived_kernel(block, x_ref, y_ref, a_ref, o_ref):
    o_ref[...] = a_ref[...]
    for source in (x_ref, y_ref):
        x = source[...]
        accumulate(0, block, 0, x[0:4], x[4:7].astype(jnp.int32), o_ref)


ACC_SHAPE = (4 * SPLITS * ROWS, COLS)


def deposit_local(payload, cells, counts):
    pick = lambda b, f: (0, jnp.maximum(b, local_start(f) // BLOCK))
    return pl.pallas_call(
        local_kernel,
        grid_spec=pltpu.PrefetchScalarGridSpec(
            num_scalar_prefetch=1,
            grid=(payload.shape[1] // BLOCK,),
            in_specs=[pl.BlockSpec((4, BLOCK), pick), pl.BlockSpec((3, BLOCK), pick)],
            out_specs=pl.BlockSpec(ACC_SHAPE, lambda b, f: (0, 0)),
        ),
        out_shape=jax.ShapeDtypeStruct(ACC_SHAPE, jnp.float32),
        compiler_params=pltpu.CompilerParams(dimension_semantics=("arbitrary",)),
    )(counts, payload, cells)


def deposit_arrived(first, second, acc, block):
    return pl.pallas_call(
        lambda x, y, a, o: arrived_kernel(block, x, y, a, o),
        grid=(1,),
        in_specs=[
            pl.BlockSpec((7, block), lambda b: (0, 0)),
            pl.BlockSpec((7, block), lambda b: (0, 0)),
            pl.BlockSpec(ACC_SHAPE, lambda b: (0, 0)),
        ],
        out_specs=pl.BlockSpec(ACC_SHAPE, lambda b: (0, 0)),
        out_shape=jax.ShapeDtypeStruct(ACC_SHAPE, jnp.float32),
        input_output_aliases={2: 0},
    )(first, second, acc)


def pack_kernel(count_ref, p_ref, c_ref, plus_x, minus_x, plus_y, minus_y):
    face = CAP_F + LANE
    corner = CAP_D + LANE
    places = (
        (plus_x, 0), (minus_x, 0), (plus_y, 0), (minus_y, 0),
        (plus_x, face), (plus_x, face + corner), (minus_x, face), (minus_x, face + corner),
    )
    start = 0
    for which, (out_ref, column) in enumerate(places):
        tally = count_ref[0, which]
        width = face if which < 4 else corner
        base = pl.multiple_of((start // LANE) * LANE, LANE)
        offset = start - base
        p = p_ref[:, pl.ds(base, width)]
        c = c_ref[:, pl.ds(base, width)]
        lane = lax.broadcasted_iota(jnp.int32, (1, width), 1)
        living = (lane >= offset) & (lane < offset + tally)
        out_ref[0:1, column : column + width] = jnp.where(living, p[0:1], 0.0)
        out_ref[1:4, column : column + width] = p[1:4]
        out_ref[4:7, column : column + width] = c.astype(jnp.float32)
        start = start + tally


def pack(payload, cells, counts):
    face = CAP_F + LANE
    corner = CAP_D + LANE
    widths = (face + 2 * corner, face + 2 * corner, face, face)
    return pl.pallas_call(
        pack_kernel,
        in_specs=[
            pl.BlockSpec(memory_space=pltpu.SMEM),
            pl.BlockSpec(memory_space=pltpu.VMEM),
            pl.BlockSpec(memory_space=pltpu.VMEM),
        ],
        out_shape=[jax.ShapeDtypeStruct((7, w), jnp.float32) for w in widths],
    )(counts, payload, cells)


def towards(block, sx, sy):
    gx = lax.axis_size("gx")
    gy = lax.axis_size("gy")
    route = []
    for ix in range(gx):
        for iy in range(gy):
            route.append((ix * gy + iy, ((ix + sx) % gx) * gy + (iy + sy) % gy))
    return lax.ppermute(block, ("gx", "gy"), route)


def bordered_density(density):
    upper_x = towards(density[:, :HALO, :], -1, 0)
    lower_x = towards(density[:, CX - HALO :, :], 1, 0)
    wide = jnp.concatenate([density, upper_x, lower_x], axis=1)
    upper_y = towards(wide[:, :, :HALO], 0, -1)
    lower_y = towards(wide[:, :, CY - HALO :], 0, 1)
    return (density, upper_x, lower_x, upper_y, lower_y)


def near(v):
    flat = jnp.zeros((1,) + v.shape[1:], v.dtype)
    up = jnp.concatenate([v[1:], flat], axis=0)
    down = jnp.concatenate([flat, v[:-1]], axis=0)
    return (
        up
        + down
        + pltpu.roll(v, WIDE_X - 1, 1)
        + pltpu.roll(v, 1, 1)
        + pltpu.roll(v, WIDE_Y - 1, 2)
        + pltpu.roll(v, 1, 2)
    )


def relax_kernel(d_ref, ux_ref, lx_ref, uy_ref, ly_ref, o_ref, b_ref):
    b_ref[...] = jnp.zeros(b_ref.shape, jnp.float32)
    b_ref[:, 0:CX, 0:CY] = d_ref[...]
    b_ref[:, CX : CX + HALO, 0:CY] = ux_ref[...]
    b_ref[:, CX + HALO :, 0:CY] = lx_ref[...]
    b_ref[:, :, CY : CY + HALO] = uy_ref[...]
    b_ref[:, :, WIDE_Y - HALO :] = ly_ref[...]
    density = b_ref[...]
    source = COUPLING * ((density + SMOOTHING * (near(density) - 6.0 * density)) - BACKGROUND)
    shape = density.shape
    parity = (
        lax.broadcasted_iota(jnp.int32, shape, 0)
        + lax.broadcasted_iota(jnp.int32, shape, 1)
        + lax.broadcasted_iota(jnp.int32, shape, 2)
    ) % 2
    residual = 0.0 - source
    slope = -6.0 - SCREENING
    field = jnp.where(parity == 0, 0.0 - residual / slope, 0.0)
    for sweep_no in range(SWEEPS):
        for colour in (0, 1):
            if sweep_no == 0 and colour == 0:
                continue
            middle = field
            residual = (
                near(middle)
                - 6.0 * middle
                - SCREENING * middle
                - CUBIC_TERM * middle * middle * middle
                - source
            )
            slope = -6.0 - SCREENING - 3.0 * CUBIC_TERM * middle * middle
            field = jnp.where(parity == colour, middle - residual / slope, middle)
    o_ref[...] = field[:, :CX, :CY]


def relax(pieces):
    return pl.pallas_call(
        relax_kernel,
        out_shape=jax.ShapeDtypeStruct((NZ, CX, CY), jnp.float32),
        scratch_shapes=[pltpu.VMEM((NZ, WIDE_X, WIDE_Y), jnp.float32)],
    )(*pieces)


def staged(payload, cells, counts):
    face = CAP_F + LANE
    corner = CAP_D + LANE
    plus_x, minus_x, plus_y, minus_y = pack(payload, cells, counts)
    from_minus_x = towards(plus_x, 1, 0)
    from_plus_x = towards(minus_x, -1, 0)
    total = deposit_local(payload, cells, counts)
    plus_y = jnp.concatenate(
        [plus_y, from_minus_x[:, face : face + corner], from_plus_x[:, face : face + corner]], axis=1
    )
    minus_y = jnp.concatenate(
        [minus_y, from_minus_x[:, face + corner :], from_plus_x[:, face + corner :]], axis=1
    )
    from_minus_y = towards(plus_y, 0, 1)
    from_plus_y = towards(minus_y, 0, -1)
    total = deposit_arrived(from_minus_x, from_plus_x, total, face)
    total = deposit_arrived(from_minus_y, from_plus_y, total, face + 2 * corner)
    total = total.reshape(SPLITS, 4, NZ // 2, CX, 2 * CY)
    summed = total[0, 0] + total[1, 0]
    density = jnp.stack([summed[..., :CY], summed[..., CY:]], axis=1).reshape(NZ, CX, CY)
    scalar_field = relax(bordered_density(density))
    summed = total[0, 1:] + total[1, 1:]
    momentum = jnp.stack([summed[..., :CY], summed[..., CY:]], axis=2).reshape(3, NZ, CX, CY)
    return (scalar_field, momentum)


def solution(mesh):
    placed = (P(None, ("gx", "gy")), P(None, ("gx", "gy")), P(("gx", "gy"), None))
    return jax.shard_map(
        staged,
        mesh=mesh,
        in_specs=placed,
        out_specs=(P(None, "gx", "gy"), P(None, None, "gx", "gy")),
        check_vma=False,
    )
```

```python
import jax
import jax.numpy as jnp
from jax import lax
from jax.experimental import pallas as pl
from jax.experimental.pallas import tpu as pltpu
from jax.sharding import PartitionSpec as P

CX = 16
CY = 128
NZ = 8
SWEEPS = 4
PART = 16384
CAP_F = 2048
CAP_D = 512


SCREENING = 0.5
CUBIC_TERM = 0.3
COUPLING = 1.5
SMOOTHING = 0.1
BACKGROUND = 1.0

HALO = 2 * SWEEPS
ROWS = 64
COLS = 256
SPLITS = 2
BLOCK = 2048
LANE = 128
WIDE_X = 2 * CX
WIDE_Y = 2 * CY


def local_start(count_ref):
    total = count_ref[0, 0]
    for edge in range(1, 8):
        total = total + count_ref[0, edge]
    return total


def accumulate(first, block, step, p, c, acc_ref):
    width = p.shape[1]
    masses = p[0:1]
    vals = jnp.concatenate([masses, masses * p[1:4]], axis=0)
    position = step * block + lax.broadcasted_iota(jnp.int32, (1, width), 1)
    row = lax.shift_right_logical(c[0:1], 1) * CX + c[1:2]
    row = jnp.where(position >= first, row, -1)
    col = lax.bitwise_and(c[0:1], 1) * CY + c[2:3]
    hi = vals.astype(jnp.bfloat16)
    lo = (vals - hi.astype(jnp.float32)).astype(jnp.bfloat16)
    parts = [q.astype(jnp.float32)[e : e + 1] for q in (hi, lo) for e in range(4)]
    row_hot = (lax.broadcasted_iota(jnp.int32, (ROWS, width), 0) == row).astype(jnp.float32)
    left = jnp.concatenate([(row_hot * part).astype(jnp.bfloat16) for part in parts], axis=0)
    right = (lax.broadcasted_iota(jnp.int32, (COLS, width), 0) == col).astype(jnp.bfloat16)
    acc_ref[...] += lax.dot_general(
        left, right, (((1,), (1,)), ((), ())), preferred_element_type=jnp.float32
    )


def local_kernel(offset, count_ref, p_ref, c_ref, *rest):
    o_ref = rest[-1]
    step = pl.program_id(0) + offset
    first = local_start(count_ref)

    @pl.when(pl.program_id(0) == 0)
    def _():
        if len(rest) == 1:
            o_ref[...] = jnp.zeros(o_ref.shape, o_ref.dtype)
        else:
            o_ref[...] = rest[0][...]

    @pl.when(step * BLOCK + BLOCK > first)
    def _():
        accumulate(first, BLOCK, step, p_ref[...], c_ref[...], o_ref)


def arrived_kernel(block, x_ref, y_ref, a_ref, o_ref):
    o_ref[...] = a_ref[...]
    for source in (x_ref, y_ref):
        x = source[...]
        accumulate(0, block, 0, x[0:4], x[4:7].astype(jnp.int32), o_ref)


ACC_SHAPE = (4 * SPLITS * ROWS, COLS)


def deposit_local(payload, cells, counts, offset, count, acc=None):
    pick = lambda b, f: (0, jnp.maximum(b + offset, local_start(f) // BLOCK))
    in_specs = [pl.BlockSpec((4, BLOCK), pick), pl.BlockSpec((3, BLOCK), pick)]
    operands = [counts, payload, cells]
    aliases = {}
    if acc is not None:
        in_specs.append(pl.BlockSpec(ACC_SHAPE, lambda b, f: (0, 0)))
        operands.append(acc)
        aliases = {3: 0}
    return pl.pallas_call(
        lambda *refs: local_kernel(offset, *refs),
        grid_spec=pltpu.PrefetchScalarGridSpec(
            num_scalar_prefetch=1,
            grid=(count,),
            in_specs=in_specs,
            out_specs=pl.BlockSpec(ACC_SHAPE, lambda b, f: (0, 0)),
        ),
        out_shape=jax.ShapeDtypeStruct(ACC_SHAPE, jnp.float32),
        input_output_aliases=aliases,
        compiler_params=pltpu.CompilerParams(dimension_semantics=("arbitrary",)),
    )(*operands)


def deposit_arrived(first, second, acc, block):
    return pl.pallas_call(
        lambda x, y, a, o: arrived_kernel(block, x, y, a, o),
        grid=(1,),
        in_specs=[
            pl.BlockSpec((7, block), lambda b: (0, 0)),
            pl.BlockSpec((7, block), lambda b: (0, 0)),
            pl.BlockSpec(ACC_SHAPE, lambda b: (0, 0)),
        ],
        out_specs=pl.BlockSpec(ACC_SHAPE, lambda b: (0, 0)),
        out_shape=jax.ShapeDtypeStruct(ACC_SHAPE, jnp.float32),
        input_output_aliases={2: 0},
    )(first, second, acc)


def pack_kernel(count_ref, p_ref, c_ref, plus_x, minus_x, plus_y, minus_y):
    face = CAP_F + LANE
    corner = CAP_D + LANE
    places = (
        (plus_x, 0), (minus_x, 0), (plus_y, 0), (minus_y, 0),
        (plus_x, face), (plus_x, face + corner), (minus_x, face), (minus_x, face + corner),
    )
    start = 0
    for which, (out_ref, column) in enumerate(places):
        tally = count_ref[0, which]
        width = face if which < 4 else corner
        base = pl.multiple_of((start // LANE) * LANE, LANE)
        offset = start - base
        p = p_ref[:, pl.ds(base, width)]
        c = c_ref[:, pl.ds(base, width)]
        lane = lax.broadcasted_iota(jnp.int32, (1, width), 1)
        living = (lane >= offset) & (lane < offset + tally)
        out_ref[0:1, column : column + width] = jnp.where(living, p[0:1], 0.0)
        out_ref[1:4, column : column + width] = p[1:4]
        out_ref[4:7, column : column + width] = c.astype(jnp.float32)
        start = start + tally


def pack(payload, cells, counts):
    face = CAP_F + LANE
    corner = CAP_D + LANE
    widths = (face + 2 * corner, face + 2 * corner, face, face)
    return pl.pallas_call(
        pack_kernel,
        in_specs=[
            pl.BlockSpec(memory_space=pltpu.SMEM),
            pl.BlockSpec(memory_space=pltpu.VMEM),
            pl.BlockSpec(memory_space=pltpu.VMEM),
        ],
        out_shape=[jax.ShapeDtypeStruct((7, w), jnp.float32) for w in widths],
    )(counts, payload, cells)


def towards(block, sx, sy):
    gx = lax.axis_size("gx")
    gy = lax.axis_size("gy")
    route = []
    for ix in range(gx):
        for iy in range(gy):
            route.append((ix * gy + iy, ((ix + sx) % gx) * gy + (iy + sy) % gy))
    return lax.ppermute(block, ("gx", "gy"), route)


def bordered_density(density):
    upper_x = towards(density[:, :HALO, :], -1, 0)
    lower_x = towards(density[:, CX - HALO :, :], 1, 0)
    wide = jnp.concatenate([density, upper_x, lower_x], axis=1)
    upper_y = towards(wide[:, :, :HALO], 0, -1)
    lower_y = towards(wide[:, :, CY - HALO :], 0, 1)
    return (density, upper_x, lower_x, upper_y, lower_y)


def near(v):
    flat = jnp.zeros((1,) + v.shape[1:], v.dtype)
    up = jnp.concatenate([v[1:], flat], axis=0)
    down = jnp.concatenate([flat, v[:-1]], axis=0)
    return (
        up
        + down
        + pltpu.roll(v, WIDE_X - 1, 1)
        + pltpu.roll(v, 1, 1)
        + pltpu.roll(v, WIDE_Y - 1, 2)
        + pltpu.roll(v, 1, 2)
    )


def relax_kernel(d_ref, ux_ref, lx_ref, uy_ref, ly_ref, o_ref, b_ref):
    b_ref[...] = jnp.zeros(b_ref.shape, jnp.float32)
    b_ref[:, 0:CX, 0:CY] = d_ref[...]
    b_ref[:, CX : CX + HALO, 0:CY] = ux_ref[...]
    b_ref[:, CX + HALO :, 0:CY] = lx_ref[...]
    b_ref[:, :, CY : CY + HALO] = uy_ref[...]
    b_ref[:, :, WIDE_Y - HALO :] = ly_ref[...]
    density = b_ref[...]
    source = COUPLING * ((density + SMOOTHING * (near(density) - 6.0 * density)) - BACKGROUND)
    shape = density.shape
    parity = (
        lax.broadcasted_iota(jnp.int32, shape, 0)
        + lax.broadcasted_iota(jnp.int32, shape, 1)
        + lax.broadcasted_iota(jnp.int32, shape, 2)
    ) % 2
    residual = 0.0 - source
    slope = -6.0 - SCREENING
    field = jnp.where(parity == 0, 0.0 - residual / slope, 0.0)
    for sweep_no in range(SWEEPS):
        for colour in (0, 1):
            if sweep_no == 0 and colour == 0:
                continue
            middle = field
            residual = (
                near(middle)
                - 6.0 * middle
                - SCREENING * middle
                - CUBIC_TERM * middle * middle * middle
                - source
            )
            slope = -6.0 - SCREENING - 3.0 * CUBIC_TERM * middle * middle
            field = jnp.where(parity == colour, middle - residual / slope, middle)
    o_ref[...] = field[:, :CX, :CY]


def relax(pieces):
    return pl.pallas_call(
        relax_kernel,
        out_shape=jax.ShapeDtypeStruct((NZ, CX, CY), jnp.float32),
        scratch_shapes=[pltpu.VMEM((NZ, WIDE_X, WIDE_Y), jnp.float32)],
    )(*pieces)


def staged(payload, cells, counts):
    face = CAP_F + LANE
    corner = CAP_D + LANE
    plus_x, minus_x, plus_y, minus_y = pack(payload, cells, counts)
    from_minus_x = towards(plus_x, 1, 0)
    from_plus_x = towards(minus_x, -1, 0)
    half = PART // BLOCK // 2
    total = deposit_local(payload, cells, counts, 0, half)
    plus_y = jnp.concatenate(
        [plus_y, from_minus_x[:, face : face + corner], from_plus_x[:, face : face + corner]], axis=1
    )
    minus_y = jnp.concatenate(
        [minus_y, from_minus_x[:, face + corner :], from_plus_x[:, face + corner :]], axis=1
    )
    from_minus_y = towards(plus_y, 0, 1)
    from_plus_y = towards(minus_y, 0, -1)
    total = deposit_local(payload, cells, counts, half, half, total)
    total = deposit_arrived(from_minus_x, from_plus_x, total, face)
    total = deposit_arrived(from_minus_y, from_plus_y, total, face + 2 * corner)
    total = total.reshape(SPLITS, 4, NZ // 2, CX, 2 * CY)
    summed = total[0, 0] + total[1, 0]
    density = jnp.stack([summed[..., :CY], summed[..., CY:]], axis=1).reshape(NZ, CX, CY)
    scalar_field = relax(bordered_density(density))
    summed = total[0, 1:] + total[1, 1:]
    momentum = jnp.stack([summed[..., :CY], summed[..., CY:]], axis=2).reshape(3, NZ, CX, CY)
    return (scalar_field, momentum)


def solution(mesh):
    placed = (P(None, ("gx", "gy")), P(None, ("gx", "gy")), P(("gx", "gy"), None))
    return jax.shard_map(
        staged,
        mesh=mesh,
        in_specs=placed,
        out_specs=(P(None, "gx", "gy"), P(None, None, "gx", "gy")),
        check_vma=False,
    )
```

```python
import jax
import jax.numpy as jnp
from jax import lax
from jax.experimental import pallas as pl
from jax.experimental.pallas import tpu as pltpu
from jax.sharding import PartitionSpec as P

CX = 16
CY = 128
NZ = 8
SWEEPS = 4
CAP_F = 2048
CAP_D = 512
MX = 2


SCREENING = 0.5
CUBIC_TERM = 0.3
COUPLING = 1.5
SMOOTHING = 0.1
BACKGROUND = 1.0

HALO = 2 * SWEEPS
ROWS = 64
COLS = 256
SPLITS = 2
BLOCK = 2048
LANE = 128
WIDE_X = 2 * CX
WIDE_Y = 2 * CY


def local_start(count_ref):
    total = count_ref[0, 0]
    for edge in range(1, 8):
        total = total + count_ref[0, edge]
    return total


def accumulate(first, block, step, p, c, acc_ref):
    width = p.shape[1]
    masses = p[0:1]
    vals = jnp.concatenate([masses, masses * p[1:4]], axis=0)
    position = step * block + lax.broadcasted_iota(jnp.int32, (1, width), 1)
    row = lax.shift_right_logical(c[0:1], 1) * CX + c[1:2]
    row = jnp.where(position >= first, row, -1)
    col = lax.bitwise_and(c[0:1], 1) * CY + c[2:3]
    hi = vals.astype(jnp.bfloat16)
    lo = (vals - hi.astype(jnp.float32)).astype(jnp.bfloat16)
    parts = [q.astype(jnp.float32)[e : e + 1] for q in (hi, lo) for e in range(4)]
    row_hot = (lax.broadcasted_iota(jnp.int32, (ROWS, width), 0) == row).astype(jnp.float32)
    left = jnp.concatenate([(row_hot * part).astype(jnp.bfloat16) for part in parts], axis=0)
    right = (lax.broadcasted_iota(jnp.int32, (COLS, width), 0) == col).astype(jnp.bfloat16)
    acc_ref[...] += lax.dot_general(
        left, right, (((1,), (1,)), ((), ())), preferred_element_type=jnp.float32
    )


def faces_kernel(x_ref, y_ref, a_ref, o_ref):
    o_ref[...] = a_ref[...]
    near_rows = NZ // 2 * MX
    for source, low in ((x_ref, 0), (y_ref, CX - MX)):
        x = source[...]
        p = x[0:4]
        c = x[4:7].astype(jnp.int32)
        width = p.shape[1]
        masses = p[0:1]
        vals = jnp.concatenate([masses, masses * p[1:4]], axis=0)
        near_i = c[1:2] - low
        row = lax.shift_right_logical(c[0:1], 1) * MX + near_i
        row = jnp.where((near_i >= 0) & (near_i < MX), row, -1)
        col = lax.bitwise_and(c[0:1], 1) * CY + c[2:3]
        hi = vals.astype(jnp.bfloat16)
        lo = (vals - hi.astype(jnp.float32)).astype(jnp.bfloat16)
        parts = [q.astype(jnp.float32)[e : e + 1] for q in (hi, lo) for e in range(4)]
        row_hot = (lax.broadcasted_iota(jnp.int32, (near_rows, width), 0) == row).astype(jnp.float32)
        left = jnp.concatenate([row_hot * part for part in parts], axis=0)
        right = (lax.broadcasted_iota(jnp.int32, (COLS, width), 0) == col).astype(jnp.float32)
        part = lax.dot_general(left, right, (((1,), (1,)), ((), ())), preferred_element_type=jnp.float32)
        for piece in range(4 * SPLITS):
            for half in range(NZ // 2):
                target = piece * ROWS + half * CX + low
                origin = piece * near_rows + half * MX
                o_ref[target : target + MX, :] += part[origin : origin + MX, :]


def deposit_faces(first, second, acc):
    block = CAP_F + LANE
    return pl.pallas_call(
        faces_kernel,
        grid=(1,),
        in_specs=[
            pl.BlockSpec((7, block), lambda b: (0, 0)),
            pl.BlockSpec((7, block), lambda b: (0, 0)),
            pl.BlockSpec(ACC_SHAPE, lambda b: (0, 0)),
        ],
        out_specs=pl.BlockSpec(ACC_SHAPE, lambda b: (0, 0)),
        out_shape=jax.ShapeDtypeStruct(ACC_SHAPE, jnp.float32),
        input_output_aliases={2: 0},
    )(first, second, acc)


def local_kernel(count_ref, p_ref, c_ref, o_ref):
    step = pl.program_id(0)
    first = local_start(count_ref)

    @pl.when(step == 0)
    def _():
        o_ref[...] = jnp.zeros(o_ref.shape, o_ref.dtype)

    @pl.when(step * BLOCK + BLOCK > first)
    def _():
        accumulate(first, BLOCK, step, p_ref[...], c_ref[...], o_ref)


def arrived_kernel(block, x_ref, y_ref, a_ref, o_ref):
    o_ref[...] = a_ref[...]
    for source in (x_ref, y_ref):
        x = source[...]
        accumulate(0, block, 0, x[0:4], x[4:7].astype(jnp.int32), o_ref)


ACC_SHAPE = (4 * SPLITS * ROWS, COLS)


def deposit_local(payload, cells, counts):
    pick = lambda b, f: (0, jnp.maximum(b, local_start(f) // BLOCK))
    return pl.pallas_call(
        local_kernel,
        grid_spec=pltpu.PrefetchScalarGridSpec(
            num_scalar_prefetch=1,
            grid=(payload.shape[1] // BLOCK,),
            in_specs=[pl.BlockSpec((4, BLOCK), pick), pl.BlockSpec((3, BLOCK), pick)],
            out_specs=pl.BlockSpec(ACC_SHAPE, lambda b, f: (0, 0)),
        ),
        out_shape=jax.ShapeDtypeStruct(ACC_SHAPE, jnp.float32),
        compiler_params=pltpu.CompilerParams(dimension_semantics=("arbitrary",)),
    )(counts, payload, cells)


def deposit_arrived(first, second, acc, block):
    return pl.pallas_call(
        lambda x, y, a, o: arrived_kernel(block, x, y, a, o),
        grid=(1,),
        in_specs=[
            pl.BlockSpec((7, block), lambda b: (0, 0)),
            pl.BlockSpec((7, block), lambda b: (0, 0)),
            pl.BlockSpec(ACC_SHAPE, lambda b: (0, 0)),
        ],
        out_specs=pl.BlockSpec(ACC_SHAPE, lambda b: (0, 0)),
        out_shape=jax.ShapeDtypeStruct(ACC_SHAPE, jnp.float32),
        input_output_aliases={2: 0},
    )(first, second, acc)


def pack_kernel(count_ref, p_ref, c_ref, plus_x, minus_x, plus_y, minus_y):
    face = CAP_F + LANE
    corner = CAP_D + LANE
    places = (
        (plus_x, 0), (minus_x, 0), (plus_y, 0), (minus_y, 0),
        (plus_x, face), (plus_x, face + corner), (minus_x, face), (minus_x, face + corner),
    )
    start = 0
    for which, (out_ref, column) in enumerate(places):
        tally = count_ref[0, which]
        width = face if which < 4 else corner
        base = pl.multiple_of((start // LANE) * LANE, LANE)
        offset = start - base
        p = p_ref[:, pl.ds(base, width)]
        c = c_ref[:, pl.ds(base, width)]
        lane = lax.broadcasted_iota(jnp.int32, (1, width), 1)
        living = (lane >= offset) & (lane < offset + tally)
        out_ref[0:1, column : column + width] = jnp.where(living, p[0:1], 0.0)
        out_ref[1:4, column : column + width] = p[1:4]
        out_ref[4:7, column : column + width] = c.astype(jnp.float32)
        start = start + tally


def pack(payload, cells, counts):
    face = CAP_F + LANE
    corner = CAP_D + LANE
    widths = (face + 2 * corner, face + 2 * corner, face, face)
    return pl.pallas_call(
        pack_kernel,
        in_specs=[
            pl.BlockSpec(memory_space=pltpu.SMEM),
            pl.BlockSpec(memory_space=pltpu.VMEM),
            pl.BlockSpec(memory_space=pltpu.VMEM),
        ],
        out_shape=[jax.ShapeDtypeStruct((7, w), jnp.float32) for w in widths],
    )(counts, payload, cells)


def towards(block, sx, sy):
    gx = lax.axis_size("gx")
    gy = lax.axis_size("gy")
    route = []
    for ix in range(gx):
        for iy in range(gy):
            route.append((ix * gy + iy, ((ix + sx) % gx) * gy + (iy + sy) % gy))
    return lax.ppermute(block, ("gx", "gy"), route)


def bordered_density(density):
    upper_x = towards(density[:, :HALO, :], -1, 0)
    lower_x = towards(density[:, CX - HALO :, :], 1, 0)
    wide = jnp.concatenate([density, upper_x, lower_x], axis=1)
    upper_y = towards(wide[:, :, :HALO], 0, -1)
    lower_y = towards(wide[:, :, CY - HALO :], 0, 1)
    return (density, upper_x, lower_x, upper_y, lower_y)


def near(v):
    flat = jnp.zeros((1,) + v.shape[1:], v.dtype)
    up = jnp.concatenate([v[1:], flat], axis=0)
    down = jnp.concatenate([flat, v[:-1]], axis=0)
    return (
        up
        + down
        + pltpu.roll(v, WIDE_X - 1, 1)
        + pltpu.roll(v, 1, 1)
        + pltpu.roll(v, WIDE_Y - 1, 2)
        + pltpu.roll(v, 1, 2)
    )


def relax_kernel(d_ref, ux_ref, lx_ref, uy_ref, ly_ref, o_ref, b_ref):
    b_ref[...] = jnp.zeros(b_ref.shape, jnp.float32)
    b_ref[:, 0:CX, 0:CY] = d_ref[...]
    b_ref[:, CX : CX + HALO, 0:CY] = ux_ref[...]
    b_ref[:, CX + HALO :, 0:CY] = lx_ref[...]
    b_ref[:, :, CY : CY + HALO] = uy_ref[...]
    b_ref[:, :, WIDE_Y - HALO :] = ly_ref[...]
    density = b_ref[...]
    source = COUPLING * ((density + SMOOTHING * (near(density) - 6.0 * density)) - BACKGROUND)
    shape = density.shape
    parity = (
        lax.broadcasted_iota(jnp.int32, shape, 0)
        + lax.broadcasted_iota(jnp.int32, shape, 1)
        + lax.broadcasted_iota(jnp.int32, shape, 2)
    ) % 2
    residual = 0.0 - source
    slope = -6.0 - SCREENING
    field = jnp.where(parity == 0, 0.0 - residual / slope, 0.0)
    for sweep_no in range(SWEEPS):
        for colour in (0, 1):
            if sweep_no == 0 and colour == 0:
                continue
            middle = field
            residual = (
                near(middle)
                - 6.0 * middle
                - SCREENING * middle
                - CUBIC_TERM * middle * middle * middle
                - source
            )
            slope = -6.0 - SCREENING - 3.0 * CUBIC_TERM * middle * middle
            field = jnp.where(parity == colour, middle - residual / slope, middle)
    o_ref[...] = field[:, :CX, :CY]


def relax(pieces):
    return pl.pallas_call(
        relax_kernel,
        out_shape=jax.ShapeDtypeStruct((NZ, CX, CY), jnp.float32),
        scratch_shapes=[pltpu.VMEM((NZ, WIDE_X, WIDE_Y), jnp.float32)],
    )(*pieces)


def staged(payload, cells, counts):
    face = CAP_F + LANE
    corner = CAP_D + LANE
    plus_x, minus_x, plus_y, minus_y = pack(payload, cells, counts)
    from_minus_x = towards(plus_x, 1, 0)
    from_plus_x = towards(minus_x, -1, 0)
    total = deposit_local(payload, cells, counts)
    plus_y = jnp.concatenate(
        [plus_y, from_minus_x[:, face : face + corner], from_plus_x[:, face : face + corner]], axis=1
    )
    minus_y = jnp.concatenate(
        [minus_y, from_minus_x[:, face + corner :], from_plus_x[:, face + corner :]], axis=1
    )
    from_minus_y = towards(plus_y, 0, 1)
    from_plus_y = towards(minus_y, 0, -1)
    total = deposit_faces(from_minus_x, from_plus_x, total)
    total = deposit_arrived(from_minus_y, from_plus_y, total, face + 2 * corner)
    total = total.reshape(SPLITS, 4, NZ // 2, CX, 2 * CY)
    summed = total[0, 0] + total[1, 0]
    density = jnp.stack([summed[..., :CY], summed[..., CY:]], axis=1).reshape(NZ, CX, CY)
    scalar_field = relax(bordered_density(density))
    summed = total[0, 1:] + total[1, 1:]
    momentum = jnp.stack([summed[..., :CY], summed[..., CY:]], axis=2).reshape(3, NZ, CX, CY)
    return (scalar_field, momentum)


def solution(mesh):
    placed = (P(None, ("gx", "gy")), P(None, ("gx", "gy")), P(("gx", "gy"), None))
    return jax.shard_map(
        staged,
        mesh=mesh,
        in_specs=placed,
        out_specs=(P(None, "gx", "gy"), P(None, None, "gx", "gy")),
        check_vma=False,
    )
```

```python
import jax
import jax.numpy as jnp
from jax import lax
from jax.experimental import pallas as pl
from jax.experimental.pallas import tpu as pltpu
from jax.sharding import PartitionSpec as P

CX = 16
CY = 128
NZ = 8
SWEEPS = 4
CAP_F = 2048
CAP_D = 512
MX = 2
MY = 16


SCREENING = 0.5
CUBIC_TERM = 0.3
COUPLING = 1.5
SMOOTHING = 0.1
BACKGROUND = 1.0

HALO = 2 * SWEEPS
ROWS = 64
COLS = 256
SPLITS = 2
BLOCK = 2048
LANE = 128
WIDE_X = 2 * CX
WIDE_Y = 2 * CY


def local_start(count_ref):
    total = count_ref[0, 0]
    for edge in range(1, 8):
        total = total + count_ref[0, edge]
    return total


def accumulate(first, block, step, p, c, acc_ref):
    width = p.shape[1]
    masses = p[0:1]
    vals = jnp.concatenate([masses, masses * p[1:4]], axis=0)
    position = step * block + lax.broadcasted_iota(jnp.int32, (1, width), 1)
    row = lax.shift_right_logical(c[0:1], 1) * CX + c[1:2]
    row = jnp.where(position >= first, row, -1)
    col = lax.bitwise_and(c[0:1], 1) * CY + c[2:3]
    hi = vals.astype(jnp.bfloat16)
    lo = (vals - hi.astype(jnp.float32)).astype(jnp.bfloat16)
    parts = [q.astype(jnp.float32)[e : e + 1] for q in (hi, lo) for e in range(4)]
    row_hot = (lax.broadcasted_iota(jnp.int32, (ROWS, width), 0) == row).astype(jnp.float32)
    left = jnp.concatenate([(row_hot * part).astype(jnp.bfloat16) for part in parts], axis=0)
    right = (lax.broadcasted_iota(jnp.int32, (COLS, width), 0) == col).astype(jnp.bfloat16)
    acc_ref[...] += lax.dot_general(
        left, right, (((1,), (1,)), ((), ())), preferred_element_type=jnp.float32
    )


def crossing_kernel(x_ref, y_ref, a_ref, o_ref):
    o_ref[...] = a_ref[...]
    for source, low in ((x_ref, 0), (y_ref, CY - MY)):
        x = source[...]
        p = x[0:4]
        c = x[4:7].astype(jnp.int32)
        width = p.shape[1]
        masses = p[0:1]
        vals = jnp.concatenate([masses, masses * p[1:4]], axis=0)
        row = lax.shift_right_logical(c[0:1], 1) * CX + c[1:2]
        near_j = c[2:3] - low
        col = lax.bitwise_and(c[0:1], 1) * MY + near_j
        col = jnp.where((near_j >= 0) & (near_j < MY), col, -1)
        hi = vals.astype(jnp.bfloat16)
        lo = (vals - hi.astype(jnp.float32)).astype(jnp.bfloat16)
        parts = [q.astype(jnp.float32)[e : e + 1] for q in (hi, lo) for e in range(4)]
        col_hot = (lax.broadcasted_iota(jnp.int32, (2 * MY, width), 0) == col).astype(jnp.float32)
        weighted = jnp.concatenate([col_hot * part for part in parts], axis=0)
        row_hot = (lax.broadcasted_iota(jnp.int32, (ROWS, width), 0) == row).astype(jnp.float32)
        part = lax.dot_general(
            row_hot, weighted, (((1,), (1,)), ((), ())), preferred_element_type=jnp.float32
        )
        for piece in range(4 * SPLITS):
            for parity in range(2):
                origin = (piece * 2 + parity) * MY
                lane = parity * CY + low
                o_ref[piece * ROWS : (piece + 1) * ROWS, lane : lane + MY] += part[:, origin : origin + MY]


def deposit_crossing(first, second, acc):
    block = first.shape[1]
    return pl.pallas_call(
        crossing_kernel,
        grid=(1,),
        in_specs=[
            pl.BlockSpec((7, block), lambda b: (0, 0)),
            pl.BlockSpec((7, block), lambda b: (0, 0)),
            pl.BlockSpec(ACC_SHAPE, lambda b: (0, 0)),
        ],
        out_specs=pl.BlockSpec(ACC_SHAPE, lambda b: (0, 0)),
        out_shape=jax.ShapeDtypeStruct(ACC_SHAPE, jnp.float32),
        input_output_aliases={2: 0},
    )(first, second, acc)


def faces_kernel(x_ref, y_ref, a_ref, o_ref):
    o_ref[...] = a_ref[...]
    near_rows = NZ // 2 * MX
    for source, low in ((x_ref, 0), (y_ref, CX - MX)):
        x = source[...]
        p = x[0:4]
        c = x[4:7].astype(jnp.int32)
        width = p.shape[1]
        masses = p[0:1]
        vals = jnp.concatenate([masses, masses * p[1:4]], axis=0)
        near_i = c[1:2] - low
        row = lax.shift_right_logical(c[0:1], 1) * MX + near_i
        row = jnp.where((near_i >= 0) & (near_i < MX), row, -1)
        col = lax.bitwise_and(c[0:1], 1) * CY + c[2:3]
        hi = vals.astype(jnp.bfloat16)
        lo = (vals - hi.astype(jnp.float32)).astype(jnp.bfloat16)
        parts = [q.astype(jnp.float32)[e : e + 1] for q in (hi, lo) for e in range(4)]
        row_hot = (lax.broadcasted_iota(jnp.int32, (near_rows, width), 0) == row).astype(jnp.float32)
        left = jnp.concatenate([row_hot * part for part in parts], axis=0)
        right = (lax.broadcasted_iota(jnp.int32, (COLS, width), 0) == col).astype(jnp.float32)
        part = lax.dot_general(left, right, (((1,), (1,)), ((), ())), preferred_element_type=jnp.float32)
        for piece in range(4 * SPLITS):
            for half in range(NZ // 2):
                target = piece * ROWS + half * CX + low
                origin = piece * near_rows + half * MX
                o_ref[target : target + MX, :] += part[origin : origin + MX, :]


def deposit_faces(first, second, acc):
    block = CAP_F + LANE
    return pl.pallas_call(
        faces_kernel,
        grid=(1,),
        in_specs=[
            pl.BlockSpec((7, block), lambda b: (0, 0)),
            pl.BlockSpec((7, block), lambda b: (0, 0)),
            pl.BlockSpec(ACC_SHAPE, lambda b: (0, 0)),
        ],
        out_specs=pl.BlockSpec(ACC_SHAPE, lambda b: (0, 0)),
        out_shape=jax.ShapeDtypeStruct(ACC_SHAPE, jnp.float32),
        input_output_aliases={2: 0},
    )(first, second, acc)


def local_kernel(count_ref, p_ref, c_ref, o_ref):
    step = pl.program_id(0)
    first = local_start(count_ref)

    @pl.when(step == 0)
    def _():
        o_ref[...] = jnp.zeros(o_ref.shape, o_ref.dtype)

    @pl.when(step * BLOCK + BLOCK > first)
    def _():
        accumulate(first, BLOCK, step, p_ref[...], c_ref[...], o_ref)


ACC_SHAPE = (4 * SPLITS * ROWS, COLS)


def deposit_local(payload, cells, counts):
    pick = lambda b, f: (0, jnp.maximum(b, local_start(f) // BLOCK))
    return pl.pallas_call(
        local_kernel,
        grid_spec=pltpu.PrefetchScalarGridSpec(
            num_scalar_prefetch=1,
            grid=(payload.shape[1] // BLOCK,),
            in_specs=[pl.BlockSpec((4, BLOCK), pick), pl.BlockSpec((3, BLOCK), pick)],
            out_specs=pl.BlockSpec(ACC_SHAPE, lambda b, f: (0, 0)),
        ),
        out_shape=jax.ShapeDtypeStruct(ACC_SHAPE, jnp.float32),
        compiler_params=pltpu.CompilerParams(dimension_semantics=("arbitrary",)),
    )(counts, payload, cells)


def pack_kernel(count_ref, p_ref, c_ref, plus_x, minus_x, plus_y, minus_y):
    face = CAP_F + LANE
    corner = CAP_D + LANE
    places = (
        (plus_x, 0), (minus_x, 0), (plus_y, 0), (minus_y, 0),
        (plus_x, face), (plus_x, face + corner), (minus_x, face), (minus_x, face + corner),
    )
    start = 0
    for which, (out_ref, column) in enumerate(places):
        tally = count_ref[0, which]
        width = face if which < 4 else corner
        base = pl.multiple_of((start // LANE) * LANE, LANE)
        offset = start - base
        p = p_ref[:, pl.ds(base, width)]
        c = c_ref[:, pl.ds(base, width)]
        lane = lax.broadcasted_iota(jnp.int32, (1, width), 1)
        living = (lane >= offset) & (lane < offset + tally)
        out_ref[0:1, column : column + width] = jnp.where(living, p[0:1], 0.0)
        out_ref[1:4, column : column + width] = p[1:4]
        out_ref[4:7, column : column + width] = c.astype(jnp.float32)
        start = start + tally


def pack(payload, cells, counts):
    face = CAP_F + LANE
    corner = CAP_D + LANE
    widths = (face + 2 * corner, face + 2 * corner, face, face)
    return pl.pallas_call(
        pack_kernel,
        in_specs=[
            pl.BlockSpec(memory_space=pltpu.SMEM),
            pl.BlockSpec(memory_space=pltpu.VMEM),
            pl.BlockSpec(memory_space=pltpu.VMEM),
        ],
        out_shape=[jax.ShapeDtypeStruct((7, w), jnp.float32) for w in widths],
    )(counts, payload, cells)


def towards(block, sx, sy):
    gx = lax.axis_size("gx")
    gy = lax.axis_size("gy")
    route = []
    for ix in range(gx):
        for iy in range(gy):
            route.append((ix * gy + iy, ((ix + sx) % gx) * gy + (iy + sy) % gy))
    return lax.ppermute(block, ("gx", "gy"), route)


def bordered_density(density):
    upper_x = towards(density[:, :HALO, :], -1, 0)
    lower_x = towards(density[:, CX - HALO :, :], 1, 0)
    wide = jnp.concatenate([density, upper_x, lower_x], axis=1)
    upper_y = towards(wide[:, :, :HALO], 0, -1)
    lower_y = towards(wide[:, :, CY - HALO :], 0, 1)
    return (density, upper_x, lower_x, upper_y, lower_y)


def near(v):
    flat = jnp.zeros((1,) + v.shape[1:], v.dtype)
    up = jnp.concatenate([v[1:], flat], axis=0)
    down = jnp.concatenate([flat, v[:-1]], axis=0)
    return (
        up
        + down
        + pltpu.roll(v, WIDE_X - 1, 1)
        + pltpu.roll(v, 1, 1)
        + pltpu.roll(v, WIDE_Y - 1, 2)
        + pltpu.roll(v, 1, 2)
    )


def relax_kernel(d_ref, ux_ref, lx_ref, uy_ref, ly_ref, o_ref, b_ref):
    b_ref[...] = jnp.zeros(b_ref.shape, jnp.float32)
    b_ref[:, 0:CX, 0:CY] = d_ref[...]
    b_ref[:, CX : CX + HALO, 0:CY] = ux_ref[...]
    b_ref[:, CX + HALO :, 0:CY] = lx_ref[...]
    b_ref[:, :, CY : CY + HALO] = uy_ref[...]
    b_ref[:, :, WIDE_Y - HALO :] = ly_ref[...]
    density = b_ref[...]
    source = COUPLING * ((density + SMOOTHING * (near(density) - 6.0 * density)) - BACKGROUND)
    shape = density.shape
    parity = (
        lax.broadcasted_iota(jnp.int32, shape, 0)
        + lax.broadcasted_iota(jnp.int32, shape, 1)
        + lax.broadcasted_iota(jnp.int32, shape, 2)
    ) % 2
    residual = 0.0 - source
    slope = -6.0 - SCREENING
    field = jnp.where(parity == 0, 0.0 - residual / slope, 0.0)
    for sweep_no in range(SWEEPS):
        for colour in (0, 1):
            if sweep_no == 0 and colour == 0:
                continue
            middle = field
            residual = (
                near(middle)
                - 6.0 * middle
                - SCREENING * middle
                - CUBIC_TERM * middle * middle * middle
                - source
            )
            slope = -6.0 - SCREENING - 3.0 * CUBIC_TERM * middle * middle
            field = jnp.where(parity == colour, middle - residual / slope, middle)
    o_ref[...] = field[:, :CX, :CY]


def relax(pieces):
    return pl.pallas_call(
        relax_kernel,
        out_shape=jax.ShapeDtypeStruct((NZ, CX, CY), jnp.float32),
        scratch_shapes=[pltpu.VMEM((NZ, WIDE_X, WIDE_Y), jnp.float32)],
    )(*pieces)


def staged(payload, cells, counts):
    face = CAP_F + LANE
    corner = CAP_D + LANE
    plus_x, minus_x, plus_y, minus_y = pack(payload, cells, counts)
    from_minus_x = towards(plus_x, 1, 0)
    from_plus_x = towards(minus_x, -1, 0)
    total = deposit_local(payload, cells, counts)
    plus_y = jnp.concatenate(
        [plus_y, from_minus_x[:, face : face + corner], from_plus_x[:, face : face + corner]], axis=1
    )
    minus_y = jnp.concatenate(
        [minus_y, from_minus_x[:, face + corner :], from_plus_x[:, face + corner :]], axis=1
    )
    from_minus_y = towards(plus_y, 0, 1)
    from_plus_y = towards(minus_y, 0, -1)
    total = deposit_faces(from_minus_x, from_plus_x, total)
    total = deposit_crossing(from_minus_y, from_plus_y, total)
    total = total.reshape(SPLITS, 4, NZ // 2, CX, 2 * CY)
    summed = total[0, 0] + total[1, 0]
    density = jnp.stack([summed[..., :CY], summed[..., CY:]], axis=1).reshape(NZ, CX, CY)
    scalar_field = relax(bordered_density(density))
    summed = total[0, 1:] + total[1, 1:]
    momentum = jnp.stack([summed[..., :CY], summed[..., CY:]], axis=2).reshape(3, NZ, CX, CY)
    return (scalar_field, momentum)


def solution(mesh):
    placed = (P(None, ("gx", "gy")), P(None, ("gx", "gy")), P(("gx", "gy"), None))
    return jax.shard_map(
        staged,
        mesh=mesh,
        in_specs=placed,
        out_specs=(P(None, "gx", "gy"), P(None, None, "gx", "gy")),
        check_vma=False,
    )
```
